32 devices in a mesh: sub: 2 (over core), row: 4 (over y, x), col: 4 (over z).
Axes of the slice: x: 2, y: 2, z: 4, core: 2. Of those that a mesh axis runs over, the one named last changes fastest.
Arguments:
- child: float32 [2, 6144, 6144], P('sub', 'row', 'col'), may hold values from -1 to 1
- row_map: int32 [2, 48], replicated, may hold values from 0 to 79, as said below
- col_map: int32 [2, 48], replicated, may hold values from 0 to 79, as said below
- own_diagonal: float32 [10240], P(('sub', 'col')), may hold values from 96 to 192
- coupling: float32 [10240, 512], P('row'), may hold values from -24 to 24
Outputs:
- factored: float32 [10240, 10240], P('row', ('sub', 'col'))
The draws below stay inside these ranges and needn't reach their ends.
Inputs may be any that keep to these rules, and one draw needn't show every extreme that they name: For each child s the entries row_map[s, :] are distinct front blocks, always including block 0 and block 79, and they rise strictly along k = (p % 12) * 4 + p // 12. col_map[s, :] holds the same set of front blocks as row_map[s, :]; they rise strictly along k = (q % 12) * 4 + (q // 12 + 1) % 4.
All inputs are finite; a program needn't handle non-finite values.
Results may differ from the reference program's by a relative error of at most 0.00005.
Values sent between devices are 32-bit elements; how exact they have to be, the bound alone decides.
No kernel may reach another device: no remote copies, remote signals or barrier semaphores. Data moves between devices by JAX's collectives and lax.ppermute only.
A program may use at most 320 MiB of HBM per device.

```python
import jax
import jax.numpy as jnp
from jax import lax

FRONT = 10240
CHILD = 6144
PANEL = 512
BLOCK = 128
FRONT_BLOCKS = 80
CHILD_BLOCKS = 48
RB_DEV = 12
CB_DEV = 12


def draw_child(key, part):
    shape = (2, CHILD, CHILD)
    return jax.random.uniform(jax.random.fold_in(key, 3), shape, jnp.float32, -1.0, 1.0)


def chosen_blocks(key, which):
    middle_blocks = jax.random.permutation(jax.random.fold_in(key, 31 + which), FRONT_BLOCKS - 2) + 1
    picked = jnp.concatenate([jnp.array([0, FRONT_BLOCKS - 1], jnp.int32), middle_blocks[:CHILD_BLOCKS - 2].astype(jnp.int32)])
    return jnp.sort(picked)


def draw_row_map(key, part):
    stride = CHILD_BLOCKS // RB_DEV
    positions = jnp.arange(CHILD_BLOCKS, dtype=jnp.int32)
    stored_order = positions % RB_DEV * stride + positions // RB_DEV
    return jnp.stack([chosen_blocks(key, 0)[stored_order], chosen_blocks(key, 1)[stored_order]]).astype(jnp.int32)


def draw_col_map(key, part):
    stride = CHILD_BLOCKS // CB_DEV
    positions = jnp.arange(CHILD_BLOCKS, dtype=jnp.int32)
    stored_order = positions % CB_DEV * stride + (positions // CB_DEV + 1) % stride
    return jnp.stack([chosen_blocks(key, 0)[stored_order], chosen_blocks(key, 1)[stored_order]]).astype(jnp.int32)


def levels(key, dims, cuts, low, high):
    gain, own = 1.0, jax.random.fold_in(key, 6)
    for axis_at, blocks in cuts:
        steps = jnp.exp(jax.random.uniform(jax.random.fold_in(own, axis_at), (blocks,), jnp.float32, low / len(cuts), high / len(cuts)))
        gain = gain * jnp.repeat(steps, dims[axis_at] // blocks).reshape([-1 if axis == axis_at else 1 for axis in range(len(dims))])
    return gain


def noise(own_key, extent, spread, reach, pieces=(), held_as=jnp.bfloat16):
    level = levels(own_key, extent, pieces, -0.22, 0.18) if pieces else 1.0
    entries = jax.random.normal(own_key, extent, jnp.float32) * spread * level
    return jnp.minimum(jnp.maximum(entries, -reach), reach).astype(held_as)


def setup_inputs(seed: int = 0) -> dict:
    seeds = jax.random.split(jax.random.key(seed), 6)
    child = draw_child(jax.random.fold_in(seeds[5], 71), 0)
    row_map = draw_row_map(jax.random.fold_in(seeds[5], 71), 0)
    col_map = draw_col_map(jax.random.fold_in(seeds[5], 71), 0)
    own_diagonal = jnp.clip(96.0 + 96.0 * jax.random.uniform(seeds[3], (FRONT,), jnp.float32) ** levels(seeds[3], (FRONT,), ((0, 8),), -0.2, 0.2), 96.0, 192.0)
    coupling = noise(seeds[4], (FRONT, PANEL), 4.0, 24.0, ((0, 4),), jnp.float32)
    return dict(child=child, row_map=row_map, col_map=col_map, own_diagonal=own_diagonal, coupling=coupling)


def reference(child, row_map, col_map, own_diagonal, coupling):
    total_blocks = FRONT // BLOCK
    front_matrix = jnp.zeros((total_blocks, BLOCK, total_blocks, BLOCK), jnp.float32)
    for which in range(2):
        contribution = child[which].reshape(CHILD_BLOCKS, BLOCK, CHILD_BLOCKS, BLOCK).transpose(0, 2, 1, 3)
        front_matrix = front_matrix.at[row_map[which][:, None], :, col_map[which][None, :], :].add(contribution)
    front_matrix = front_matrix.reshape(FRONT, FRONT)
    diagonal_index = jnp.arange(FRONT, dtype=jnp.int32)
    front_matrix = front_matrix.at[diagonal_index, diagonal_index].add(own_diagonal)
    front_matrix = front_matrix.at[PANEL:, :PANEL].add(coupling[PANEL:])
    corner = front_matrix[:PANEL, :PANEL]
    symmetric = jnp.tril(corner) + jnp.tril(corner, -1).T
    lower = jnp.linalg.cholesky(symmetric)
    below = jax.scipy.linalg.solve_triangular(lower, front_matrix[PANEL:, :PANEL].T, lower=True).T
    trailing = front_matrix[PANEL:, PANEL:] - jnp.dot(below, below.T, precision=lax.Precision.HIGHEST)
    upper_rows = jnp.concatenate([lower, jnp.zeros((PANEL, FRONT - PANEL), jnp.float32)], axis=1)
    lower_rows = jnp.concatenate([below, trailing], axis=1)
    return jnp.concatenate([upper_rows, lower_rows], axis=0)
```

```python
import jax
import jax.numpy as jnp
from jax import lax
from jax.sharding import PartitionSpec as P

FRONT = 10240
PANEL = 512
BLOCK = 128


def from_root(value, axis, source):
    kept = jnp.where(lax.axis_index(axis) == source, value, 0).astype(value.dtype)
    return lax.psum(kept, axis)


def block_routes(parent_blocks, per_source, per_target):
    number = parent_blocks.shape[0]
    positions = jnp.arange(number, dtype=jnp.int32)
    source = positions // per_source
    target = parent_blocks // per_target
    earlier = (
        (source[:, None] == source[None, :])
        & (target[:, None] == target[None, :])
        & (positions[None, :] < positions[:, None])
    )
    slot_index = jnp.sum(earlier.astype(jnp.int32), axis=1)
    return (positions, source, target, slot_index, parent_blocks % per_target)


def sending_table(parent_blocks, own_index, per_source, per_target, targets, capacity):
    positions, source, target, slot_index, local_block = block_routes(
        parent_blocks, per_source, per_target
    )
    wanted = jnp.arange(targets * capacity, dtype=jnp.int32)
    matches = (source == own_index)[None, :] & (
        (target * capacity + slot_index)[None, :] == wanted[:, None]
    )
    within = positions % per_source
    return jnp.where(
        jnp.any(matches, axis=1),
        jnp.sum(jnp.where(matches, within[None, :], 0), axis=1),
        per_source,
    )


def receiving_table(parent_blocks, own_index, per_source, per_target, capacity, offset, empty_slot):
    positions, source, target, slot_index, local_block = block_routes(
        parent_blocks, per_source, per_target
    )
    wanted = jnp.arange(per_target, dtype=jnp.int32)
    matches = (target == own_index)[None, :] & (local_block[None, :] == wanted[:, None])
    flat_slot = (source + offset) * capacity + slot_index
    return jnp.where(
        jnp.any(matches, axis=1),
        jnp.sum(jnp.where(matches, flat_slot[None, :], 0), axis=1),
        empty_slot,
    )


def with_zero(blocks, axis):
    shape = list(blocks.shape)
    shape[axis] = 1
    return jnp.concatenate([blocks, jnp.zeros(shape, blocks.dtype)], axis=axis)


def symmetric_of(corner):
    return jnp.tril(corner) + jnp.tril(corner, -1).T


def factor_corner(corner):
    lower = jnp.linalg.cholesky(symmetric_of(corner))
    inverse = jax.scipy.linalg.solve_triangular(
        lower, jnp.eye(PANEL, dtype=jnp.float32), lower=True
    )
    return (lower, inverse)


def apply_inverse(rows, inverse):
    return lax.dot_general(rows, inverse, (((1,), (1,)), ((), ())), precision=lax.Precision.HIGHEST)


def early_corner(child_piece, row_map, col_map, own_diagonal):
    n_row = lax.axis_size("row")
    n_col = lax.axis_size("col")
    n_sub = lax.axis_size("sub")
    rows_here, cols_here = child_piece.shape
    row_blocks = rows_here // BLOCK
    col_blocks = cols_here // BLOCK
    panel_blocks = PANEL // BLOCK
    first_rows = min(row_blocks, -(-panel_blocks // n_row))
    first_cols = min(col_blocks, -(-panel_blocks // n_col))
    piece = child_piece[: first_rows * BLOCK, : first_cols * BLOCK]
    pieces = lax.all_gather(piece, ("sub", "row", "col"))
    pieces = pieces.reshape(n_sub, n_row, n_col, first_rows, BLOCK, first_cols, BLOCK)
    pieces = pieces.transpose(0, 1, 3, 2, 5, 4, 6).reshape(
        n_sub, n_row * first_rows, n_col * first_cols, BLOCK, BLOCK
    )
    row_pos = (
        jnp.arange(n_row, dtype=jnp.int32)[:, None] * row_blocks
        + jnp.arange(first_rows, dtype=jnp.int32)[None, :]
    ).reshape(-1)
    col_pos = (
        jnp.arange(n_col, dtype=jnp.int32)[:, None] * col_blocks
        + jnp.arange(first_cols, dtype=jnp.int32)[None, :]
    ).reshape(-1)
    corner = jnp.zeros((panel_blocks + 1, panel_blocks + 1, BLOCK, BLOCK), jnp.float32)
    for which in range(n_sub):
        rb = row_map[which][row_pos]
        cb = col_map[which][col_pos]
        rb = jnp.where(rb < panel_blocks, rb, panel_blocks)
        cb = jnp.where(cb < panel_blocks, cb, panel_blocks)
        corner = corner.at[rb[:, None], cb[None, :]].add(pieces[which])
    corner = corner[:panel_blocks, :panel_blocks].transpose(0, 2, 1, 3).reshape(PANEL, PANEL)
    diagonal = lax.all_gather(own_diagonal, ("sub", "col"), tiled=True)[:PANEL]
    return corner + jnp.diag(diagonal)


def shards(child, row_map, col_map, own_diagonal, coupling):
    n_row = lax.axis_size("row")
    n_col = lax.axis_size("col")
    n_group = lax.axis_size(("sub", "col"))
    my_row = lax.axis_index("row")
    my_col = lax.axis_index("col")
    my_sub = lax.axis_index("sub")
    my_group = lax.axis_index(("sub", "col"))
    child_piece = child[0]
    rows_here, cols_here = child_piece.shape
    front_rows = FRONT // n_row
    front_cols = FRONT // n_group
    row_blocks = rows_here // BLOCK
    col_blocks = cols_here // BLOCK
    front_row_blocks = front_rows // BLOCK
    front_col_blocks = front_cols // BLOCK
    row_cap = min(row_blocks, (front_row_blocks + n_row - 1) // n_row)
    col_cap = min(col_blocks, (front_col_blocks + n_col - 1) // n_col)
    n_children = row_map.shape[0]
    my_rows_map = lax.dynamic_index_in_dim(row_map, my_sub, 0, keepdims=False)
    my_cols_map = lax.dynamic_index_in_dim(col_map, my_sub, 0, keepdims=False)

    corner = early_corner(child_piece, row_map, col_map, own_diagonal)
    lower, inverse = factor_corner(corner)

    by_col = child_piece.reshape(rows_here, col_blocks, BLOCK).transpose(1, 0, 2)
    by_col = with_zero(by_col, 0)
    chosen = sending_table(my_cols_map, my_col, col_blocks, front_col_blocks, n_group, col_cap)
    outgoing = jnp.take(by_col, chosen, axis=0).reshape(n_group, col_cap, rows_here, BLOCK)
    arrived = lax.all_to_all(outgoing, ("sub", "col"), split_axis=0, concat_axis=0, tiled=True)
    arrived = with_zero(arrived.reshape(n_group * col_cap, rows_here, BLOCK), 0)
    per_child = []
    for which in range(n_children):
        placement = receiving_table(
            col_map[which],
            my_group,
            col_blocks,
            front_col_blocks,
            col_cap,
            which * n_col,
            n_group * col_cap,
        )
        placed = jnp.take(arrived, placement, axis=0)
        placed = placed.reshape(front_col_blocks, row_blocks, BLOCK, BLOCK)
        per_child.append(with_zero(placed, 1))

    sent = []
    for which in range(n_children):
        chosen = sending_table(row_map[which], my_row, row_blocks, front_row_blocks, n_row, row_cap)
        sent.append(jnp.take(per_child[which], chosen, axis=1))
    outgoing = jnp.stack(sent, axis=0).reshape(
        n_children, front_col_blocks, n_row, row_cap, BLOCK, BLOCK
    )
    outgoing = outgoing.transpose(2, 0, 1, 3, 4, 5)
    arrived = lax.all_to_all(outgoing, "row", split_axis=0, concat_axis=0, tiled=True)
    arrived = arrived.reshape(n_row, n_children, front_col_blocks, row_cap, BLOCK, BLOCK)
    assembled = jnp.zeros((front_col_blocks, front_row_blocks, BLOCK, BLOCK), jnp.float32)
    for which in range(n_children):
        from_child = arrived[:, which].transpose(1, 0, 2, 3, 4).reshape(
            front_col_blocks, n_row * row_cap, BLOCK, BLOCK
        )
        from_child = with_zero(from_child, 1)
        placement = receiving_table(
            row_map[which], my_row, row_blocks, front_row_blocks, row_cap, 0, n_row * row_cap
        )
        assembled = assembled + jnp.take(from_child, placement, axis=1)
    assembled = assembled.transpose(1, 2, 0, 3).reshape(front_rows, front_cols)

    global_row = my_row * front_rows + jnp.arange(front_rows, dtype=jnp.int32)
    global_col = my_group * front_cols + jnp.arange(front_cols, dtype=jnp.int32)
    on_diagonal = global_row[:, None] == global_col[None, :]
    assembled = assembled + jnp.where(on_diagonal, own_diagonal[None, :], 0.0)
    coupling_wide = jnp.concatenate(
        [coupling, jnp.zeros((front_rows, front_cols - PANEL), jnp.float32)], axis=1
    )
    coupling_mask = (global_row[:, None] >= PANEL) & (global_col[None, :] < PANEL)
    front_part = assembled + jnp.where(coupling_mask, coupling_wide, 0.0)
    panel_cols = front_part[:, :PANEL]
    theirs_start = my_group * front_cols % front_rows
    theirs_root = my_group * front_cols // front_rows
    own_rows = apply_inverse(panel_cols, inverse)
    top_rows = jnp.where(my_row == 0, lower, own_rows[:PANEL])
    own_rows = jnp.concatenate([top_rows, own_rows[PANEL:]], axis=0)
    own_rows = from_root(own_rows, ("sub", "col"), 0)
    theirs = from_root(own_rows, "row", theirs_root)
    theirs = lax.dynamic_slice_in_dim(theirs, theirs_start, front_cols, 0)
    update = lax.dot_general(
        own_rows, theirs, (((1,), (1,)), ((), ())), precision=lax.Precision.HIGHEST
    )
    panel_wide = jnp.concatenate(
        [own_rows, jnp.zeros((front_rows, front_cols - PANEL), jnp.float32)], axis=1
    )
    trailing = front_part - update
    result = jnp.where(
        global_col[None, :] < PANEL,
        panel_wide,
        jnp.where(global_row[:, None] < PANEL, 0.0, trailing),
    )
    return result


def solution(mesh):
    placed = (P("sub", "row", "col"), P(), P(), P(("sub", "col")), P("row", None))
    return jax.shard_map(
        shards, mesh=mesh, in_specs=placed, out_specs=P("row", ("sub", "col")), check_vma=False
    )
```

```python
import jax
import jax.numpy as jnp
from jax import lax
from jax.sharding import PartitionSpec as P

FRONT = 10240
PANEL = 512
BLOCK = 128


def from_root(value, axis, source):
    kept = jnp.where(lax.axis_index(axis) == source, value, 0).astype(value.dtype)
    return lax.psum(kept, axis)


def block_routes(parent_blocks, per_source, per_target):
    number = parent_blocks.shape[0]
    positions = jnp.arange(number, dtype=jnp.int32)
    source = positions // per_source
    target = parent_blocks // per_target
    earlier = (
        (source[:, None] == source[None, :])
        & (target[:, None] == target[None, :])
        & (positions[None, :] < positions[:, None])
    )
    slot_index = jnp.sum(earlier.astype(jnp.int32), axis=1)
    return (positions, source, target, slot_index, parent_blocks % per_target)


def sending_table(parent_blocks, own_index, per_source, per_target, targets, capacity):
    positions, source, target, slot_index, local_block = block_routes(
        parent_blocks, per_source, per_target
    )
    wanted = jnp.arange(targets * capacity, dtype=jnp.int32)
    matches = (source == own_index)[None, :] & (
        (target * capacity + slot_index)[None, :] == wanted[:, None]
    )
    within = positions % per_source
    return jnp.where(
        jnp.any(matches, axis=1),
        jnp.sum(jnp.where(matches, within[None, :], 0), axis=1),
        per_source,
    )


def receiving_table(parent_blocks, own_index, per_source, per_target, capacity, offset, empty_slot):
    positions, source, target, slot_index, local_block = block_routes(
        parent_blocks, per_source, per_target
    )
    wanted = jnp.arange(per_target, dtype=jnp.int32)
    matches = (target == own_index)[None, :] & (local_block[None, :] == wanted[:, None])
    flat_slot = (source + offset) * capacity + slot_index
    return jnp.where(
        jnp.any(matches, axis=1),
        jnp.sum(jnp.where(matches, flat_slot[None, :], 0), axis=1),
        empty_slot,
    )


def with_zero(blocks, axis):
    shape = list(blocks.shape)
    shape[axis] = 1
    return jnp.concatenate([blocks, jnp.zeros(shape, blocks.dtype)], axis=axis)


def symmetric_of(corner):
    return jnp.tril(corner) + jnp.tril(corner, -1).T


def factor_corner(corner):
    lower = jnp.linalg.cholesky(symmetric_of(corner))
    inverse = jax.scipy.linalg.solve_triangular(
        lower, jnp.eye(PANEL, dtype=jnp.float32), lower=True
    )
    return (lower, inverse)


def apply_inverse(rows, inverse):
    return lax.dot_general(rows, inverse, (((1,), (1,)), ((), ())), precision=lax.Precision.HIGHEST)


def early_corner(child_piece, row_map, col_map, own_diagonal):
    n_row = lax.axis_size("row")
    n_col = lax.axis_size("col")
    n_sub = lax.axis_size("sub")
    rows_here, cols_here = child_piece.shape
    row_blocks = rows_here // BLOCK
    col_blocks = cols_here // BLOCK
    panel_blocks = PANEL // BLOCK
    first_rows = min(row_blocks, -(-panel_blocks // n_row))
    first_cols = min(col_blocks, -(-panel_blocks // n_col))
    piece = child_piece[: first_rows * BLOCK, : first_cols * BLOCK]
    pieces = lax.all_gather(piece, ("sub", "row", "col"))
    pieces = pieces.reshape(n_sub, n_row, n_col, first_rows, BLOCK, first_cols, BLOCK)
    pieces = pieces.transpose(0, 1, 3, 2, 5, 4, 6).reshape(
        n_sub, n_row * first_rows, n_col * first_cols, BLOCK, BLOCK
    )
    row_pos = (
        jnp.arange(n_row, dtype=jnp.int32)[:, None] * row_blocks
        + jnp.arange(first_rows, dtype=jnp.int32)[None, :]
    ).reshape(-1)
    col_pos = (
        jnp.arange(n_col, dtype=jnp.int32)[:, None] * col_blocks
        + jnp.arange(first_cols, dtype=jnp.int32)[None, :]
    ).reshape(-1)
    corner = jnp.zeros((panel_blocks + 1, panel_blocks + 1, BLOCK, BLOCK), jnp.float32)
    for which in range(n_sub):
        rb = row_map[which][row_pos]
        cb = col_map[which][col_pos]
        rb = jnp.where(rb < panel_blocks, rb, panel_blocks)
        cb = jnp.where(cb < panel_blocks, cb, panel_blocks)
        corner = corner.at[rb[:, None], cb[None, :]].add(pieces[which])
    corner = corner[:panel_blocks, :panel_blocks].transpose(0, 2, 1, 3).reshape(PANEL, PANEL)
    diagonal = lax.all_gather(own_diagonal, ("sub", "col"), tiled=True)[:PANEL]
    return corner + jnp.diag(diagonal)


def shards(child, row_map, col_map, own_diagonal, coupling):
    n_row = lax.axis_size("row")
    n_col = lax.axis_size("col")
    n_group = lax.axis_size(("sub", "col"))
    my_row = lax.axis_index("row")
    my_col = lax.axis_index("col")
    my_sub = lax.axis_index("sub")
    my_group = lax.axis_index(("sub", "col"))
    child_piece = child[0]
    rows_here, cols_here = child_piece.shape
    front_rows = FRONT // n_row
    front_cols = FRONT // n_group
    row_blocks = rows_here // BLOCK
    col_blocks = cols_here // BLOCK
    front_row_blocks = front_rows // BLOCK
    front_col_blocks = front_cols // BLOCK
    row_cap = min(row_blocks, (front_row_blocks + n_row - 1) // n_row)
    col_cap = min(col_blocks, (front_col_blocks + n_col - 1) // n_col)
    n_children = row_map.shape[0]
    my_rows_map = lax.dynamic_index_in_dim(row_map, my_sub, 0, keepdims=False)
    my_cols_map = lax.dynamic_index_in_dim(col_map, my_sub, 0, keepdims=False)

    corner = early_corner(child_piece, row_map, col_map, own_diagonal)

    by_col = child_piece.reshape(rows_here, col_blocks, BLOCK)
    chosen = sending_table(my_cols_map, my_col, col_blocks, front_col_blocks, n_group, col_cap)
    outgoing = jnp.take(by_col, chosen, axis=1, mode="fill", fill_value=0.0)
    outgoing = outgoing.transpose(1, 0, 2).reshape(n_group, col_cap, rows_here, BLOCK)
    outgoing, corner = lax.optimization_barrier((outgoing, corner))
    lower, inverse = factor_corner(corner)
    arrived = lax.all_to_all(outgoing, ("sub", "col"), split_axis=0, concat_axis=0, tiled=True)
    arrived, lower, inverse = lax.optimization_barrier((arrived, lower, inverse))
    arrived = arrived.reshape(n_group * col_cap, row_blocks, BLOCK, BLOCK)

    col_index = jnp.stack(
        [
            receiving_table(
                col_map[which],
                my_group,
                col_blocks,
                front_col_blocks,
                col_cap,
                which * n_col,
                n_group * col_cap,
            )
            for which in range(n_children)
        ]
    )
    row_index = jnp.stack(
        [
            sending_table(row_map[which], my_row, row_blocks, front_row_blocks, n_row, row_cap)
            for which in range(n_children)
        ]
    ).reshape(n_children, n_row, row_cap)
    outgoing = arrived.at[
        col_index[None, :, None, :], row_index.transpose(1, 0, 2)[:, :, :, None]
    ].get(mode="fill", fill_value=0.0)
    arrived = lax.all_to_all(outgoing, "row", split_axis=0, concat_axis=0, tiled=True)
    arrived = arrived.transpose(1, 0, 2, 3, 4, 5).reshape(
        n_children, n_row * row_cap, front_col_blocks, BLOCK, BLOCK
    )
    assembled = None
    for which in range(n_children):
        placement = receiving_table(
            row_map[which], my_row, row_blocks, front_row_blocks, row_cap, 0, n_row * row_cap
        )
        part = arrived[which].at[placement].get(mode="fill", fill_value=0.0)
        assembled = part if assembled is None else assembled + part
    assembled = assembled.transpose(0, 2, 1, 3).reshape(front_rows, front_cols)

    global_row = my_row * front_rows + jnp.arange(front_rows, dtype=jnp.int32)
    global_col = my_group * front_cols + jnp.arange(front_cols, dtype=jnp.int32)
    on_diagonal = global_row[:, None] == global_col[None, :]
    assembled = assembled + jnp.where(on_diagonal, own_diagonal[None, :], 0.0)
    coupling_wide = jnp.concatenate(
        [coupling, jnp.zeros((front_rows, front_cols - PANEL), jnp.float32)], axis=1
    )
    coupling_mask = (global_row[:, None] >= PANEL) & (global_col[None, :] < PANEL)
    front_part = assembled + jnp.where(coupling_mask, coupling_wide, 0.0)
    panel_cols = front_part[:, :PANEL]
    theirs_start = my_group * front_cols % front_rows
    theirs_root = my_group * front_cols // front_rows
    own_rows = apply_inverse(panel_cols, inverse)
    top_rows = jnp.where(my_row == 0, lower, own_rows[:PANEL])
    own_rows = jnp.concatenate([top_rows, own_rows[PANEL:]], axis=0)
    own_rows = from_root(own_rows, ("sub", "col"), 0)
    theirs = from_root(own_rows, "row", theirs_root)
    theirs = lax.dynamic_slice_in_dim(theirs, theirs_start, front_cols, 0)
    update = lax.dot_general(
        own_rows, theirs, (((1,), (1,)), ((), ())), precision=lax.Precision.HIGHEST
    )
    panel_wide = jnp.concatenate(
        [own_rows, jnp.zeros((front_rows, front_cols - PANEL), jnp.float32)], axis=1
    )
    trailing = front_part - update
    result = jnp.where(
        global_col[None, :] < PANEL,
        panel_wide,
        jnp.where(global_row[:, None] < PANEL, 0.0, trailing),
    )
    return result


def solution(mesh):
    placed = (P("sub", "row", "col"), P(), P(), P(("sub", "col")), P("row", None))
    return jax.shard_map(
        shards, mesh=mesh, in_specs=placed, out_specs=P("row", ("sub", "col")), check_vma=False
    )
```

```python
import jax
import jax.numpy as jnp
from jax import lax
from jax.sharding import PartitionSpec as P

FRONT = 10240
PANEL = 512
BLOCK = 128


def from_root(value, axis, source):
    kept = jnp.where(lax.axis_index(axis) == source, value, 0).astype(value.dtype)
    return lax.psum(kept, axis)


def block_routes(parent_blocks, per_source, per_target):
    number = parent_blocks.shape[0]
    positions = jnp.arange(number, dtype=jnp.int32)
    source = positions // per_source
    target = parent_blocks // per_target
    earlier = (
        (source[:, None] == source[None, :])
        & (target[:, None] == target[None, :])
        & (positions[None, :] < positions[:, None])
    )
    slot_index = jnp.sum(earlier.astype(jnp.int32), axis=1)
    return (positions, source, target, slot_index, parent_blocks % per_target)


def sending_table(parent_blocks, own_index, per_source, per_target, targets, capacity):
    positions, source, target, slot_index, local_block = block_routes(
        parent_blocks, per_source, per_target
    )
    wanted = jnp.arange(targets * capacity, dtype=jnp.int32)
    matches = (source == own_index)[None, :] & (
        (target * capacity + slot_index)[None, :] == wanted[:, None]
    )
    within = positions % per_source
    return jnp.where(
        jnp.any(matches, axis=1),
        jnp.sum(jnp.where(matches, within[None, :], 0), axis=1),
        per_source,
    )


def receiving_table(parent_blocks, own_index, per_source, per_target, capacity, offset, empty_slot):
    positions, source, target, slot_index, local_block = block_routes(
        parent_blocks, per_source, per_target
    )
    wanted = jnp.arange(per_target, dtype=jnp.int32)
    matches = (target == own_index)[None, :] & (local_block[None, :] == wanted[:, None])
    flat_slot = (source + offset) * capacity + slot_index
    return jnp.where(
        jnp.any(matches, axis=1),
        jnp.sum(jnp.where(matches, flat_slot[None, :], 0), axis=1),
        empty_slot,
    )


def with_zero(blocks, axis):
    shape = list(blocks.shape)
    shape[axis] = 1
    return jnp.concatenate([blocks, jnp.zeros(shape, blocks.dtype)], axis=axis)


def symmetric_of(corner):
    return jnp.tril(corner) + jnp.tril(corner, -1).T


def factor_corner(corner):
    lower = jnp.linalg.cholesky(symmetric_of(corner))
    inverse = jax.scipy.linalg.solve_triangular(
        lower, jnp.eye(PANEL, dtype=jnp.float32), lower=True
    )
    return (lower, inverse)


def apply_inverse(rows, inverse):
    return lax.dot_general(rows, inverse, (((1,), (1,)), ((), ())), precision=lax.Precision.HIGHEST)


def early_corner(child_piece, row_map, col_map, own_diagonal):
    n_row = lax.axis_size("row")
    n_col = lax.axis_size("col")
    n_sub = lax.axis_size("sub")
    rows_here, cols_here = child_piece.shape
    row_blocks = rows_here // BLOCK
    col_blocks = cols_here // BLOCK
    panel_blocks = PANEL // BLOCK
    first_rows = min(row_blocks, -(-panel_blocks // n_row))
    first_cols = min(col_blocks, -(-panel_blocks // n_col))
    piece = child_piece[: first_rows * BLOCK, : first_cols * BLOCK]
    pieces = lax.all_gather(piece, ("sub", "row", "col"))
    pieces = pieces.reshape(n_sub, n_row, n_col, first_rows, BLOCK, first_cols, BLOCK)
    pieces = pieces.transpose(0, 1, 3, 2, 5, 4, 6).reshape(
        n_sub, n_row * first_rows, n_col * first_cols, BLOCK, BLOCK
    )
    row_pos = (
        jnp.arange(n_row, dtype=jnp.int32)[:, None] * row_blocks
        + jnp.arange(first_rows, dtype=jnp.int32)[None, :]
    ).reshape(-1)
    col_pos = (
        jnp.arange(n_col, dtype=jnp.int32)[:, None] * col_blocks
        + jnp.arange(first_cols, dtype=jnp.int32)[None, :]
    ).reshape(-1)
    corner = jnp.zeros((panel_blocks + 1, panel_blocks + 1, BLOCK, BLOCK), jnp.float32)
    for which in range(n_sub):
        rb = row_map[which][row_pos]
        cb = col_map[which][col_pos]
        rb = jnp.where(rb < panel_blocks, rb, panel_blocks)
        cb = jnp.where(cb < panel_blocks, cb, panel_blocks)
        corner = corner.at[rb[:, None], cb[None, :]].add(pieces[which])
    corner = corner[:panel_blocks, :panel_blocks].transpose(0, 2, 1, 3).reshape(PANEL, PANEL)
    diagonal = lax.all_gather(own_diagonal, ("sub", "col"), tiled=True)[:PANEL]
    return corner + jnp.diag(diagonal)


def shards(child, row_map, col_map, own_diagonal, coupling):
    n_row = lax.axis_size("row")
    n_col = lax.axis_size("col")
    n_group = lax.axis_size(("sub", "col"))
    my_row = lax.axis_index("row")
    my_col = lax.axis_index("col")
    my_sub = lax.axis_index("sub")
    my_group = lax.axis_index(("sub", "col"))
    child_piece = child[0]
    rows_here, cols_here = child_piece.shape
    front_rows = FRONT // n_row
    front_cols = FRONT // n_group
    row_blocks = rows_here // BLOCK
    col_blocks = cols_here // BLOCK
    front_row_blocks = front_rows // BLOCK
    front_col_blocks = front_cols // BLOCK
    row_cap = min(row_blocks, (front_row_blocks + n_row - 1) // n_row)
    col_cap = min(col_blocks, (front_col_blocks + n_col - 1) // n_col)
    n_children = row_map.shape[0]
    my_rows_map = lax.dynamic_index_in_dim(row_map, my_sub, 0, keepdims=False)
    my_cols_map = lax.dynamic_index_in_dim(col_map, my_sub, 0, keepdims=False)

    corner = early_corner(child_piece, row_map, col_map, own_diagonal)

    by_col = child_piece.reshape(rows_here, col_blocks, BLOCK)
    chosen = sending_table(my_cols_map, my_col, col_blocks, front_col_blocks, n_group, col_cap)
    outgoing = jnp.take(by_col, chosen, axis=1, mode="fill", fill_value=0.0)
    outgoing = outgoing.transpose(1, 0, 2).reshape(n_group, col_cap, rows_here, BLOCK)
    outgoing, corner = lax.optimization_barrier((outgoing, corner))
    lower, inverse = factor_corner(corner)
    arrived = lax.all_to_all(outgoing, ("sub", "col"), split_axis=0, concat_axis=0, tiled=True)
    arrived, lower, inverse = lax.optimization_barrier((arrived, lower, inverse))
    arrived = arrived.reshape(n_group * col_cap, row_blocks, BLOCK, BLOCK)

    col_index = jnp.stack(
        [
            receiving_table(
                col_map[which],
                my_group,
                col_blocks,
                front_col_blocks,
                col_cap,
                which * n_col,
                n_group * col_cap,
            )
            for which in range(n_children)
        ]
    )
    row_index = jnp.stack(
        [
            sending_table(row_map[which], my_row, row_blocks, front_row_blocks, n_row, row_cap)
            for which in range(n_children)
        ]
    ).reshape(n_children, n_row, row_cap)
    outgoing = arrived.at[
        col_index[None, :, None, :], row_index.transpose(1, 0, 2)[:, :, :, None]
    ].get(mode="fill", fill_value=0.0)
    arrived = lax.all_to_all(outgoing, "row", split_axis=0, concat_axis=0, tiled=True)
    arrived = arrived.transpose(1, 0, 2, 3, 4, 5).reshape(
        n_children, n_row * row_cap, front_col_blocks, BLOCK, BLOCK
    )
    assembled = None
    for which in range(n_children):
        placement = receiving_table(
            row_map[which], my_row, row_blocks, front_row_blocks, row_cap, 0, n_row * row_cap
        )
        part = arrived[which].at[placement].get(mode="fill", fill_value=0.0)
        assembled = part if assembled is None else assembled + part
    assembled = assembled.transpose(0, 2, 1, 3).reshape(front_rows, front_cols)

    global_row = my_row * front_rows + jnp.arange(front_rows, dtype=jnp.int32)
    global_col = my_group * front_cols + jnp.arange(front_cols, dtype=jnp.int32)
    on_diagonal = global_row[:, None] == global_col[None, :]
    assembled = assembled + jnp.where(on_diagonal, own_diagonal[None, :], 0.0)
    coupling_wide = jnp.concatenate(
        [coupling, jnp.zeros((front_rows, front_cols - PANEL), jnp.float32)], axis=1
    )
    coupling_mask = (global_row[:, None] >= PANEL) & (global_col[None, :] < PANEL)
    front_part = assembled + jnp.where(coupling_mask, coupling_wide, 0.0)
    panel_cols = front_part[:, :PANEL]
    theirs_start = my_group * front_cols % front_rows
    theirs_root = my_group * front_cols // front_rows
    own_rows = apply_inverse(panel_cols, inverse)
    top_rows = jnp.where(my_row == 0, lower, own_rows[:PANEL])
    own_rows = jnp.concatenate([top_rows, own_rows[PANEL:]], axis=0)
    own_rows = from_root(own_rows, ("sub", "col"), 0)
    theirs = lax.dynamic_slice_in_dim(own_rows, theirs_start, front_cols, 0)
    theirs = from_root(theirs, "row", theirs_root)
    update = lax.dot_general(
        own_rows, theirs, (((1,), (1,)), ((), ())), precision=lax.Precision.HIGHEST
    )
    panel_wide = jnp.concatenate(
        [own_rows, jnp.zeros((front_rows, front_cols - PANEL), jnp.float32)], axis=1
    )
    trailing = front_part - update
    result = jnp.where(
        global_col[None, :] < PANEL,
        panel_wide,
        jnp.where(global_row[:, None] < PANEL, 0.0, trailing),
    )
    return result


def solution(mesh):
    placed = (P("sub", "row", "col"), P(), P(), P(("sub", "col")), P("row", None))
    return jax.shard_map(
        shards, mesh=mesh, in_specs=placed, out_specs=P("row", ("sub", "col")), check_vma=False
    )
```

```python
import jax
import jax.numpy as jnp
from jax import lax
from jax.sharding import PartitionSpec as P

FRONT = 10240
PANEL = 512
BLOCK = 128


def from_root(value, axis, source):
    kept = jnp.where(lax.axis_index(axis) == source, value, 0).astype(value.dtype)
    return lax.psum(kept, axis)


def block_routes(parent_blocks, per_source, per_target):
    number = parent_blocks.shape[0]
    positions = jnp.arange(number, dtype=jnp.int32)
    source = positions // per_source
    target = parent_blocks // per_target
    earlier = (
        (source[:, None] == source[None, :])
        & (target[:, None] == target[None, :])
        & (positions[None, :] < positions[:, None])
    )
    slot_index = jnp.sum(earlier.astype(jnp.int32), axis=1)
    return (positions, source, target, slot_index, parent_blocks % per_target)


def sending_table(parent_blocks, own_index, per_source, per_target, targets, capacity):
    positions, source, target, slot_index, local_block = block_routes(
        parent_blocks, per_source, per_target
    )
    wanted = jnp.arange(targets * capacity, dtype=jnp.int32)
    matches = (source == own_index)[None, :] & (
        (target * capacity + slot_index)[None, :] == wanted[:, None]
    )
    within = positions % per_source
    return jnp.where(
        jnp.any(matches, axis=1),
        jnp.sum(jnp.where(matches, within[None, :], 0), axis=1),
        per_source,
    )


def receiving_table(parent_blocks, own_index, per_source, per_target, capacity, offset, empty_slot):
    positions, source, target, slot_index, local_block = block_routes(
        parent_blocks, per_source, per_target
    )
    wanted = jnp.arange(per_target, dtype=jnp.int32)
    matches = (target == own_index)[None, :] & (local_block[None, :] == wanted[:, None])
    flat_slot = (source + offset) * capacity + slot_index
    return jnp.where(
        jnp.any(matches, axis=1),
        jnp.sum(jnp.where(matches, flat_slot[None, :], 0), axis=1),
        empty_slot,
    )


def with_zero(blocks, axis):
    shape = list(blocks.shape)
    shape[axis] = 1
    return jnp.concatenate([blocks, jnp.zeros(shape, blocks.dtype)], axis=axis)


def symmetric_of(corner):
    return jnp.tril(corner) + jnp.tril(corner, -1).T


def factor_corner(corner):
    lower = jnp.linalg.cholesky(symmetric_of(corner))
    inverse = jax.scipy.linalg.solve_triangular(
        lower, jnp.eye(PANEL, dtype=jnp.float32), lower=True
    )
    return (lower, inverse)


def apply_inverse(rows, inverse):
    return lax.dot_general(rows, inverse, (((1,), (1,)), ((), ())), precision=lax.Precision.HIGHEST)


def early_corner(child_piece, row_map, col_map, own_diagonal):
    n_row = lax.axis_size("row")
    n_col = lax.axis_size("col")
    n_sub = lax.axis_size("sub")
    rows_here, cols_here = child_piece.shape
    row_blocks = rows_here // BLOCK
    col_blocks = cols_here // BLOCK
    panel_blocks = PANEL // BLOCK
    first_rows = min(row_blocks, -(-panel_blocks // n_row))
    first_cols = min(col_blocks, -(-panel_blocks // n_col))
    piece = child_piece[: first_rows * BLOCK, : first_cols * BLOCK]
    pieces = lax.all_gather(piece, ("sub", "row", "col"))
    pieces = pieces.reshape(n_sub, n_row, n_col, first_rows, BLOCK, first_cols, BLOCK)
    pieces = pieces.transpose(0, 1, 3, 2, 5, 4, 6).reshape(
        n_sub, n_row * first_rows, n_col * first_cols, BLOCK, BLOCK
    )
    row_pos = (
        jnp.arange(n_row, dtype=jnp.int32)[:, None] * row_blocks
        + jnp.arange(first_rows, dtype=jnp.int32)[None, :]
    ).reshape(-1)
    col_pos = (
        jnp.arange(n_col, dtype=jnp.int32)[:, None] * col_blocks
        + jnp.arange(first_cols, dtype=jnp.int32)[None, :]
    ).reshape(-1)
    corner = jnp.zeros((panel_blocks + 1, panel_blocks + 1, BLOCK, BLOCK), jnp.float32)
    for which in range(n_sub):
        rb = row_map[which][row_pos]
        cb = col_map[which][col_pos]
        rb = jnp.where(rb < panel_blocks, rb, panel_blocks)
        cb = jnp.where(cb < panel_blocks, cb, panel_blocks)
        corner = corner.at[rb[:, None], cb[None, :]].add(pieces[which])
    corner = corner[:panel_blocks, :panel_blocks].transpose(0, 2, 1, 3).reshape(PANEL, PANEL)
    diagonal = lax.all_gather(own_diagonal, ("sub", "col"), tiled=True)[:PANEL]
    return corner + jnp.diag(diagonal)


def shards(child, row_map, col_map, own_diagonal, coupling):
    n_row = lax.axis_size("row")
    n_col = lax.axis_size("col")
    n_group = lax.axis_size(("sub", "col"))
    my_row = lax.axis_index("row")
    my_col = lax.axis_index("col")
    my_sub = lax.axis_index("sub")
    my_group = lax.axis_index(("sub", "col"))
    child_piece = child[0]
    rows_here, cols_here = child_piece.shape
    front_rows = FRONT // n_row
    front_cols = FRONT // n_group
    row_blocks = rows_here // BLOCK
    col_blocks = cols_here // BLOCK
    front_row_blocks = front_rows // BLOCK
    front_col_blocks = front_cols // BLOCK
    row_cap = min(row_blocks, (front_row_blocks + n_row - 1) // n_row)
    col_cap = min(col_blocks, (front_col_blocks + n_col - 1) // n_col)
    n_sub = lax.axis_size("sub")
    my_rows_map = lax.dynamic_index_in_dim(row_map, my_sub, 0, keepdims=False)
    my_cols_map = lax.dynamic_index_in_dim(col_map, my_sub, 0, keepdims=False)

    corner = early_corner(child_piece, row_map, col_map, own_diagonal)

    by_col = child_piece.reshape(rows_here, col_blocks, BLOCK)
    chosen = sending_table(my_cols_map, my_col, col_blocks, front_col_blocks, n_group, col_cap)
    chosen = jnp.minimum(chosen, col_blocks - 1).reshape(n_sub, n_col * col_cap)
    chosen = jnp.stack([chosen[1 - my_sub], chosen[my_sub]]).reshape(-1)
    outgoing = by_col.at[:, chosen].get(mode="promise_in_bounds")
    outgoing = outgoing.transpose(1, 0, 2).reshape(2, n_col, col_cap, rows_here, BLOCK)
    outgoing, corner = lax.optimization_barrier((outgoing, corner))
    lower, inverse = factor_corner(corner)
    other_half = lax.all_to_all(outgoing[0], "col", split_axis=0, concat_axis=0, tiled=True)
    other_half = lax.ppermute(other_half, "sub", [(0, 1), (1, 0)])

    def row_sending(half, which):
        cols_of = lax.dynamic_index_in_dim(col_map, which, 0, keepdims=False)
        rows_of = lax.dynamic_index_in_dim(row_map, which, 0, keepdims=False)
        col_index = receiving_table(
            cols_of, my_group, col_blocks, front_col_blocks, col_cap, 0, n_col * col_cap
        )
        col_valid = col_index < n_col * col_cap
        col_index = jnp.minimum(col_index, n_col * col_cap - 1)
        row_index = sending_table(rows_of, my_row, row_blocks, front_row_blocks, n_row, row_cap)
        row_index = jnp.minimum(row_index, row_blocks - 1).reshape(n_row, row_cap)
        half = half.reshape(n_col * col_cap, row_blocks, BLOCK, BLOCK)
        sending = half.at[col_index[None, None, :], row_index[:, :, None]].get(
            mode="promise_in_bounds"
        )
        return sending, col_valid, rows_of

    def row_receiving(sending, col_valid, rows_of):
        pieces = [lax.dynamic_index_in_dim(sending, my_row, 0, keepdims=False)]
        for shift in range(1, n_row):
            piece = lax.dynamic_index_in_dim(sending, (my_row + shift) % n_row, 0, keepdims=False)
            pairs = [(i, (i + shift) % n_row) for i in range(n_row)]
            pieces.append(lax.ppermute(piece, "row", pairs))
        received = jnp.stack(pieces).reshape(n_row * row_cap, front_col_blocks, BLOCK, BLOCK)
        placement = receiving_table(
            rows_of, my_row, row_blocks, front_row_blocks, row_cap, 0, n_row * row_cap
        )
        row_valid = placement < n_row * row_cap
        source = jnp.minimum(placement, n_row * row_cap - 1) // row_cap
        slot = placement % row_cap
        placement = ((my_row - source) % n_row) * row_cap + slot
        part = received.at[placement].get(mode="promise_in_bounds")
        keep = row_valid[:, None] & col_valid[None, :]
        return part, keep

    sending_other, col_valid_other, rows_other = row_sending(other_half, 1 - my_sub)
    sending_other, own_outgoing = lax.optimization_barrier((sending_other, outgoing[1]))
    part_other, keep_other = row_receiving(sending_other, col_valid_other, rows_other)
    own_half = lax.all_to_all(own_outgoing, "col", split_axis=0, concat_axis=0, tiled=True)
    own_half, lower, inverse = lax.optimization_barrier((own_half, lower, inverse))
    sending_own, col_valid_own, rows_own = row_sending(own_half, my_sub)
    part_own, keep_own = row_receiving(sending_own, col_valid_own, rows_own)
    assembled = jnp.where(keep_other[:, :, None, None], part_other, 0.0) + jnp.where(
        keep_own[:, :, None, None], part_own, 0.0
    )
    assembled = assembled.transpose(0, 2, 1, 3).reshape(front_rows, front_cols)

    global_row = my_row * front_rows + jnp.arange(front_rows, dtype=jnp.int32)
    global_col = my_group * front_cols + jnp.arange(front_cols, dtype=jnp.int32)
    on_diagonal = global_row[:, None] == global_col[None, :]
    assembled = assembled + jnp.where(on_diagonal, own_diagonal[None, :], 0.0)
    coupling_wide = jnp.concatenate(
        [coupling, jnp.zeros((front_rows, front_cols - PANEL), jnp.float32)], axis=1
    )
    coupling_mask = (global_row[:, None] >= PANEL) & (global_col[None, :] < PANEL)
    front_part = assembled + jnp.where(coupling_mask, coupling_wide, 0.0)
    panel_cols = front_part[:, :PANEL]
    theirs_start = my_group * front_cols % front_rows
    theirs_root = my_group * front_cols // front_rows
    own_rows = apply_inverse(panel_cols, inverse)
    top_rows = jnp.where(my_row == 0, lower, own_rows[:PANEL])
    own_rows = jnp.concatenate([top_rows, own_rows[PANEL:]], axis=0)
    own_rows = from_root(own_rows, ("sub", "col"), 0)
    theirs = lax.dynamic_slice_in_dim(own_rows, theirs_start, front_cols, 0)
    theirs = from_root(theirs, "row", theirs_root)
    update = lax.dot_general(
        own_rows, theirs, (((1,), (1,)), ((), ())), precision=lax.Precision.HIGHEST
    )
    panel_wide = jnp.concatenate(
        [own_rows, jnp.zeros((front_rows, front_cols - PANEL), jnp.float32)], axis=1
    )
    trailing = front_part - update
    result = jnp.where(
        global_col[None, :] < PANEL,
        panel_wide,
        jnp.where(global_row[:, None] < PANEL, 0.0, trailing),
    )
    return result


def solution(mesh):
    placed = (P("sub", "row", "col"), P(), P(), P(("sub", "col")), P("row", None))
    return jax.shard_map(
        shards, mesh=mesh, in_specs=placed, out_specs=P("row", ("sub", "col")), check_vma=False
    )
```

```python
import jax
import jax.numpy as jnp
from jax import lax
from jax.sharding import PartitionSpec as P

FRONT = 10240
PANEL = 512
BLOCK = 128


def from_root(value, axis, source):
    kept = jnp.where(lax.axis_index(axis) == source, value, 0).astype(value.dtype)
    return lax.psum(kept, axis)


def block_routes(parent_blocks, per_source, per_target):
    number = parent_blocks.shape[0]
    positions = jnp.arange(number, dtype=jnp.int32)
    source = positions // per_source
    target = parent_blocks // per_target
    earlier = (
        (source[:, None] == source[None, :])
        & (target[:, None] == target[None, :])
        & (positions[None, :] < positions[:, None])
    )
    slot_index = jnp.sum(earlier.astype(jnp.int32), axis=1)
    return (positions, source, target, slot_index, parent_blocks % per_target)


def sending_table(parent_blocks, own_index, per_source, per_target, targets, capacity):
    positions, source, target, slot_index, local_block = block_routes(
        parent_blocks, per_source, per_target
    )
    wanted = jnp.arange(targets * capacity, dtype=jnp.int32)
    matches = (source == own_index)[None, :] & (
        (target * capacity + slot_index)[None, :] == wanted[:, None]
    )
    within = positions % per_source
    return jnp.where(
        jnp.any(matches, axis=1),
        jnp.sum(jnp.where(matches, within[None, :], 0), axis=1),
        per_source,
    )


def receiving_table(parent_blocks, own_index, per_source, per_target, capacity, offset, empty_slot):
    positions, source, target, slot_index, local_block = block_routes(
        parent_blocks, per_source, per_target
    )
    wanted = jnp.arange(per_target, dtype=jnp.int32)
    matches = (target == own_index)[None, :] & (local_block[None, :] == wanted[:, None])
    flat_slot = (source + offset) * capacity + slot_index
    return jnp.where(
        jnp.any(matches, axis=1),
        jnp.sum(jnp.where(matches, flat_slot[None, :], 0), axis=1),
        empty_slot,
    )


def with_zero(blocks, axis):
    shape = list(blocks.shape)
    shape[axis] = 1
    return jnp.concatenate([blocks, jnp.zeros(shape, blocks.dtype)], axis=axis)


def symmetric_of(corner):
    return jnp.tril(corner) + jnp.tril(corner, -1).T


def factor_corner(corner):
    lower = jnp.linalg.cholesky(symmetric_of(corner))
    inverse = jax.scipy.linalg.solve_triangular(
        lower, jnp.eye(PANEL, dtype=jnp.float32), lower=True
    )
    return (lower, inverse)


def apply_inverse(rows, inverse):
    return lax.dot_general(rows, inverse, (((1,), (1,)), ((), ())), precision=lax.Precision.HIGHEST)


def early_corner(child_piece, row_map, col_map, full_diagonal):
    n_row = lax.axis_size("row")
    n_col = lax.axis_size("col")
    n_sub = lax.axis_size("sub")
    rows_here, cols_here = child_piece.shape
    row_blocks = rows_here // BLOCK
    col_blocks = cols_here // BLOCK
    panel_blocks = PANEL // BLOCK
    first_rows = min(row_blocks, -(-panel_blocks // n_row))
    first_cols = min(col_blocks, -(-panel_blocks // n_col))
    piece = child_piece[: first_rows * BLOCK, : first_cols * BLOCK]
    pieces = lax.all_gather(piece, ("sub", "row", "col"))
    pieces = pieces.reshape(n_sub, n_row, n_col, first_rows, BLOCK, first_cols, BLOCK)
    pieces = pieces.transpose(0, 1, 3, 2, 5, 4, 6).reshape(
        n_sub, n_row * first_rows, n_col * first_cols, BLOCK, BLOCK
    )
    row_pos = (
        jnp.arange(n_row, dtype=jnp.int32)[:, None] * row_blocks
        + jnp.arange(first_rows, dtype=jnp.int32)[None, :]
    ).reshape(-1)
    col_pos = (
        jnp.arange(n_col, dtype=jnp.int32)[:, None] * col_blocks
        + jnp.arange(first_cols, dtype=jnp.int32)[None, :]
    ).reshape(-1)
    corner = jnp.zeros((panel_blocks + 1, panel_blocks + 1, BLOCK, BLOCK), jnp.float32)
    for which in range(n_sub):
        rb = row_map[which][row_pos]
        cb = col_map[which][col_pos]
        rb = jnp.where(rb < panel_blocks, rb, panel_blocks)
        cb = jnp.where(cb < panel_blocks, cb, panel_blocks)
        corner = corner.at[rb[:, None], cb[None, :]].add(pieces[which])
    corner = corner[:panel_blocks, :panel_blocks].transpose(0, 2, 1, 3).reshape(PANEL, PANEL)
    return corner + jnp.diag(full_diagonal[:PANEL])


def shards(child, row_map, col_map, own_diagonal, coupling):
    n_row = lax.axis_size("row")
    n_col = lax.axis_size("col")
    n_group = lax.axis_size(("sub", "col"))
    my_row = lax.axis_index("row")
    my_col = lax.axis_index("col")
    my_sub = lax.axis_index("sub")
    my_group = lax.axis_index(("sub", "col"))
    child_piece = child[0]
    rows_here, cols_here = child_piece.shape
    front_rows = FRONT // n_row
    front_cols = FRONT // n_group
    row_blocks = rows_here // BLOCK
    col_blocks = cols_here // BLOCK
    front_row_blocks = front_rows // BLOCK
    front_col_blocks = front_cols // BLOCK
    row_cap = min(row_blocks, (front_row_blocks + n_row - 1) // n_row)
    col_cap = min(col_blocks, (front_col_blocks + n_col - 1) // n_col)
    n_sub = lax.axis_size("sub")
    my_rows_map = lax.dynamic_index_in_dim(row_map, my_sub, 0, keepdims=False)
    my_cols_map = lax.dynamic_index_in_dim(col_map, my_sub, 0, keepdims=False)

    full_diagonal = lax.all_gather(own_diagonal, ("sub", "col"), tiled=True)
    corner = early_corner(child_piece, row_map, col_map, full_diagonal)
    global_row = my_row * front_rows + jnp.arange(front_rows, dtype=jnp.int32)

    panel_blocks = PANEL // BLOCK
    first_cols = min(col_blocks, -(-panel_blocks // n_col))
    cands = lax.all_gather(child_piece[:, : first_cols * BLOCK], ("sub", "col"))
    cands = cands.reshape(n_sub, n_col, rows_here, first_cols, BLOCK).transpose(0, 1, 3, 2, 4)
    cands = cands.reshape(n_sub, n_col * first_cols, rows_here, BLOCK)
    cand_pos = (
        jnp.arange(n_col, dtype=jnp.int32)[:, None] * col_blocks
        + jnp.arange(first_cols, dtype=jnp.int32)[None, :]
    ).reshape(-1)
    panel_send = []
    for which in range(n_sub):
        found = col_map[which][cand_pos][None, :] == jnp.arange(panel_blocks, dtype=jnp.int32)[:, None]
        pick = jnp.argmax(found, axis=1)
        stored = jnp.where(jnp.any(found, axis=1)[:, None, None], cands[which][pick], 0.0)
        stored = stored.reshape(panel_blocks, row_blocks, BLOCK, BLOCK)
        pick_rows = sending_table(row_map[which], my_row, row_blocks, front_row_blocks, n_row, row_cap)
        pick_rows = jnp.minimum(pick_rows, row_blocks - 1).reshape(n_row, row_cap)
        panel_send.append(stored.at[:, pick_rows].get(mode="promise_in_bounds"))
    panel_send = jnp.stack(panel_send).transpose(2, 0, 3, 1, 4, 5)
    pieces = [lax.dynamic_index_in_dim(panel_send, my_row, 0, keepdims=False)]
    for shift in range(1, n_row):
        piece = lax.dynamic_index_in_dim(panel_send, (my_row + shift) % n_row, 0, keepdims=False)
        pieces.append(lax.ppermute(piece, "row", [(i, (i + shift) % n_row) for i in range(n_row)]))
    panel_got = jnp.stack(pieces)
    panel_rows = None
    for which in range(n_sub):
        placement = receiving_table(
            row_map[which], my_row, row_blocks, front_row_blocks, row_cap, 0, n_row * row_cap
        )
        row_valid = placement < n_row * row_cap
        source = jnp.minimum(placement, n_row * row_cap - 1) // row_cap
        placement = ((my_row - source) % n_row) * row_cap + placement % row_cap
        got = panel_got[:, which].reshape(n_row * row_cap, panel_blocks, BLOCK, BLOCK)
        got = jnp.where(row_valid[:, None, None, None], got.at[placement].get(mode="promise_in_bounds"), 0.0)
        panel_rows = got if panel_rows is None else panel_rows + got
    panel_rows = panel_rows.transpose(0, 2, 1, 3).reshape(front_rows, PANEL)
    panel_rows = panel_rows + jnp.where(global_row[:, None] >= PANEL, coupling, 0.0)
    panel_rows = panel_rows + jnp.where(
        global_row[:, None] == jnp.arange(PANEL, dtype=jnp.int32)[None, :], full_diagonal[None, :PANEL], 0.0
    )

    by_col = child_piece.reshape(rows_here, col_blocks, BLOCK)
    chosen = sending_table(my_cols_map, my_col, col_blocks, front_col_blocks, n_group, col_cap)
    chosen = jnp.minimum(chosen, col_blocks - 1).reshape(n_sub, n_col * col_cap)
    chosen = jnp.stack([chosen[1 - my_sub], chosen[my_sub]]).reshape(-1)
    outgoing = by_col.at[:, chosen].get(mode="promise_in_bounds")
    outgoing = outgoing.transpose(1, 0, 2).reshape(2, n_col, col_cap, rows_here, BLOCK)
    outgoing, corner = lax.optimization_barrier((outgoing, corner))
    lower, inverse = factor_corner(corner)
    other_half = lax.all_to_all(outgoing[0], "col", split_axis=0, concat_axis=0, tiled=True)
    other_half = lax.ppermute(other_half, "sub", [(0, 1), (1, 0)])

    def row_sending(half, which):
        cols_of = lax.dynamic_index_in_dim(col_map, which, 0, keepdims=False)
        rows_of = lax.dynamic_index_in_dim(row_map, which, 0, keepdims=False)
        col_index = receiving_table(
            cols_of, my_group, col_blocks, front_col_blocks, col_cap, 0, n_col * col_cap
        )
        col_valid = col_index < n_col * col_cap
        col_index = jnp.minimum(col_index, n_col * col_cap - 1)
        row_index = sending_table(rows_of, my_row, row_blocks, front_row_blocks, n_row, row_cap)
        row_index = jnp.minimum(row_index, row_blocks - 1).reshape(n_row, row_cap)
        half = half.reshape(n_col * col_cap, row_blocks, BLOCK, BLOCK)
        sending = half.at[col_index[None, None, :], row_index[:, :, None]].get(
            mode="promise_in_bounds"
        )
        return sending, col_valid, rows_of

    def row_receiving(sending, col_valid, rows_of):
        pieces = [lax.dynamic_index_in_dim(sending, my_row, 0, keepdims=False)]
        for shift in range(1, n_row):
            piece = lax.dynamic_index_in_dim(sending, (my_row + shift) % n_row, 0, keepdims=False)
            pairs = [(i, (i + shift) % n_row) for i in range(n_row)]
            pieces.append(lax.ppermute(piece, "row", pairs))
        received = jnp.stack(pieces).reshape(n_row * row_cap, front_col_blocks, BLOCK, BLOCK)
        placement = receiving_table(
            rows_of, my_row, row_blocks, front_row_blocks, row_cap, 0, n_row * row_cap
        )
        row_valid = placement < n_row * row_cap
        source = jnp.minimum(placement, n_row * row_cap - 1) // row_cap
        slot = placement % row_cap
        placement = ((my_row - source) % n_row) * row_cap + slot
        part = received.at[placement].get(mode="promise_in_bounds")
        keep = row_valid[:, None] & col_valid[None, :]
        return part, keep

    sending_other, col_valid_other, rows_other = row_sending(other_half, 1 - my_sub)
    sending_other, own_outgoing = lax.optimization_barrier((sending_other, outgoing[1]))
    part_other, keep_other = row_receiving(sending_other, col_valid_other, rows_other)
    own_half = lax.all_to_all(own_outgoing, "col", split_axis=0, concat_axis=0, tiled=True)
    own_half, lower, inverse = lax.optimization_barrier((own_half, lower, inverse))
    sending_own, col_valid_own, rows_own = row_sending(own_half, my_sub)
    part_own, keep_own = row_receiving(sending_own, col_valid_own, rows_own)
    assembled = jnp.where(keep_other[:, :, None, None], part_other, 0.0) + jnp.where(
        keep_own[:, :, None, None], part_own, 0.0
    )
    assembled = assembled.transpose(0, 2, 1, 3).reshape(front_rows, front_cols)

    global_col = my_group * front_cols + jnp.arange(front_cols, dtype=jnp.int32)
    on_diagonal = global_row[:, None] == global_col[None, :]
    assembled = assembled + jnp.where(on_diagonal, own_diagonal[None, :], 0.0)
    coupling_wide = jnp.concatenate(
        [coupling, jnp.zeros((front_rows, front_cols - PANEL), jnp.float32)], axis=1
    )
    coupling_mask = (global_row[:, None] >= PANEL) & (global_col[None, :] < PANEL)
    front_part = assembled + jnp.where(coupling_mask, coupling_wide, 0.0)
    theirs_start = my_group * front_cols % front_rows
    theirs_root = my_group * front_cols // front_rows
    own_rows = apply_inverse(panel_rows, inverse)
    top_rows = jnp.where(my_row == 0, lower, own_rows[:PANEL])
    own_rows = jnp.concatenate([top_rows, own_rows[PANEL:]], axis=0)
    theirs = lax.dynamic_slice_in_dim(own_rows, theirs_start, front_cols, 0)
    theirs = from_root(theirs, "row", theirs_root)
    update = lax.dot_general(
        own_rows, theirs, (((1,), (1,)), ((), ())), precision=lax.Precision.HIGHEST
    )
    panel_wide = jnp.concatenate(
        [own_rows, jnp.zeros((front_rows, front_cols - PANEL), jnp.float32)], axis=1
    )
    trailing = front_part - update
    result = jnp.where(
        global_col[None, :] < PANEL,
        panel_wide,
        jnp.where(global_row[:, None] < PANEL, 0.0, trailing),
    )
    return result


def solution(mesh):
    placed = (P("sub", "row", "col"), P(), P(), P(("sub", "col")), P("row", None))
    return jax.shard_map(
        shards, mesh=mesh, in_specs=placed, out_specs=P("row", ("sub", "col")), check_vma=False
    )
```

```python
import jax
import jax.numpy as jnp
from jax import lax
from jax.sharding import PartitionSpec as P

FRONT = 10240
PANEL = 512
BLOCK = 128


def from_root(value, axis, source):
    kept = jnp.where(lax.axis_index(axis) == source, value, 0).astype(value.dtype)
    return lax.psum(kept, axis)


def block_routes(parent_blocks, per_source, per_target):
    number = parent_blocks.shape[0]
    positions = jnp.arange(number, dtype=jnp.int32)
    source = positions // per_source
    target = parent_blocks // per_target
    earlier = (
        (source[:, None] == source[None, :])
        & (target[:, None] == target[None, :])
        & (positions[None, :] < positions[:, None])
    )
    slot_index = jnp.sum(earlier.astype(jnp.int32), axis=1)
    return (positions, source, target, slot_index, parent_blocks % per_target)


def sending_table(parent_blocks, own_index, per_source, per_target, targets, capacity):
    positions, source, target, slot_index, local_block = block_routes(
        parent_blocks, per_source, per_target
    )
    wanted = jnp.arange(targets * capacity, dtype=jnp.int32)
    matches = (source == own_index)[None, :] & (
        (target * capacity + slot_index)[None, :] == wanted[:, None]
    )
    within = positions % per_source
    return jnp.where(
        jnp.any(matches, axis=1),
        jnp.sum(jnp.where(matches, within[None, :], 0), axis=1),
        per_source,
    )


def receiving_table(parent_blocks, own_index, per_source, per_target, capacity, offset, empty_slot):
    positions, source, target, slot_index, local_block = block_routes(
        parent_blocks, per_source, per_target
    )
    wanted = jnp.arange(per_target, dtype=jnp.int32)
    matches = (target == own_index)[None, :] & (local_block[None, :] == wanted[:, None])
    flat_slot = (source + offset) * capacity + slot_index
    return jnp.where(
        jnp.any(matches, axis=1),
        jnp.sum(jnp.where(matches, flat_slot[None, :], 0), axis=1),
        empty_slot,
    )


def with_zero(blocks, axis):
    shape = list(blocks.shape)
    shape[axis] = 1
    return jnp.concatenate([blocks, jnp.zeros(shape, blocks.dtype)], axis=axis)


def symmetric_of(corner):
    return jnp.tril(corner) + jnp.tril(corner, -1).T


def factor_corner(corner):
    lower = jnp.linalg.cholesky(symmetric_of(corner))
    inverse = jax.scipy.linalg.solve_triangular(
        lower, jnp.eye(PANEL, dtype=jnp.float32), lower=True
    )
    return (lower, inverse)


def apply_inverse(rows, inverse):
    return lax.dot_general(rows, inverse, (((1,), (1,)), ((), ())), precision=lax.Precision.HIGHEST)


def early_corner(child_piece, row_map, col_map, full_diagonal):
    n_row = lax.axis_size("row")
    n_col = lax.axis_size("col")
    n_sub = lax.axis_size("sub")
    rows_here, cols_here = child_piece.shape
    row_blocks = rows_here // BLOCK
    col_blocks = cols_here // BLOCK
    panel_blocks = PANEL // BLOCK
    first_rows = min(row_blocks, -(-panel_blocks // n_row))
    first_cols = min(col_blocks, -(-panel_blocks // n_col))
    piece = child_piece[: first_rows * BLOCK, : first_cols * BLOCK]
    pieces = lax.all_gather(piece, ("sub", "row", "col"))
    pieces = pieces.reshape(n_sub, n_row, n_col, first_rows, BLOCK, first_cols, BLOCK)
    pieces = pieces.transpose(0, 1, 3, 2, 5, 4, 6).reshape(
        n_sub, n_row * first_rows, n_col * first_cols, BLOCK, BLOCK
    )
    row_pos = (
        jnp.arange(n_row, dtype=jnp.int32)[:, None] * row_blocks
        + jnp.arange(first_rows, dtype=jnp.int32)[None, :]
    ).reshape(-1)
    col_pos = (
        jnp.arange(n_col, dtype=jnp.int32)[:, None] * col_blocks
        + jnp.arange(first_cols, dtype=jnp.int32)[None, :]
    ).reshape(-1)
    corner = jnp.zeros((panel_blocks + 1, panel_blocks + 1, BLOCK, BLOCK), jnp.float32)
    for which in range(n_sub):
        rb = row_map[which][row_pos]
        cb = col_map[which][col_pos]
        rb = jnp.where(rb < panel_blocks, rb, panel_blocks)
        cb = jnp.where(cb < panel_blocks, cb, panel_blocks)
        corner = corner.at[rb[:, None], cb[None, :]].add(pieces[which])
    corner = corner[:panel_blocks, :panel_blocks].transpose(0, 2, 1, 3).reshape(PANEL, PANEL)
    return corner + jnp.diag(full_diagonal[:PANEL])


def shards(child, row_map, col_map, own_diagonal, coupling):
    n_row = lax.axis_size("row")
    n_col = lax.axis_size("col")
    n_group = lax.axis_size(("sub", "col"))
    my_row = lax.axis_index("row")
    my_col = lax.axis_index("col")
    my_sub = lax.axis_index("sub")
    my_group = lax.axis_index(("sub", "col"))
    child_piece = child[0]
    rows_here, cols_here = child_piece.shape
    front_rows = FRONT // n_row
    front_cols = FRONT // n_group
    row_blocks = rows_here // BLOCK
    col_blocks = cols_here // BLOCK
    front_row_blocks = front_rows // BLOCK
    front_col_blocks = front_cols // BLOCK
    row_cap = min(row_blocks, (front_row_blocks + n_row - 1) // n_row)
    col_cap = min(col_blocks, (front_col_blocks + n_col - 1) // n_col)
    n_sub = lax.axis_size("sub")
    my_rows_map = lax.dynamic_index_in_dim(row_map, my_sub, 0, keepdims=False)
    my_cols_map = lax.dynamic_index_in_dim(col_map, my_sub, 0, keepdims=False)

    full_diagonal = lax.all_gather(own_diagonal, ("sub", "col"), tiled=True)
    corner = early_corner(child_piece, row_map, col_map, full_diagonal)
    global_row = my_row * front_rows + jnp.arange(front_rows, dtype=jnp.int32)

    panel_blocks = PANEL // BLOCK
    first_cols = min(col_blocks, -(-panel_blocks // n_col))
    cands = lax.all_gather(child_piece[:, : first_cols * BLOCK], ("sub", "col"))
    cands = cands.reshape(n_sub, n_col, rows_here, first_cols, BLOCK).transpose(0, 1, 3, 2, 4)
    cands = cands.reshape(n_sub, n_col * first_cols, rows_here, BLOCK)
    cand_pos = (
        jnp.arange(n_col, dtype=jnp.int32)[:, None] * col_blocks
        + jnp.arange(first_cols, dtype=jnp.int32)[None, :]
    ).reshape(-1)
    panel_send = []
    for which in range(n_sub):
        found = col_map[which][cand_pos][None, :] == jnp.arange(panel_blocks, dtype=jnp.int32)[:, None]
        pick = jnp.argmax(found, axis=1)
        stored = jnp.where(jnp.any(found, axis=1)[:, None, None], cands[which][pick], 0.0)
        stored = stored.reshape(panel_blocks, row_blocks, BLOCK, BLOCK)
        pick_rows = sending_table(row_map[which], my_row, row_blocks, front_row_blocks, n_row, row_cap)
        pick_rows = jnp.minimum(pick_rows, row_blocks - 1).reshape(n_row, row_cap)
        panel_send.append(stored.at[:, pick_rows].get(mode="promise_in_bounds"))
    panel_send = jnp.stack(panel_send).transpose(2, 0, 3, 1, 4, 5)

    by_col = child_piece.reshape(rows_here, col_blocks, BLOCK)
    chosen = sending_table(my_cols_map, my_col, col_blocks, front_col_blocks, n_group, col_cap)
    chosen = jnp.minimum(chosen, col_blocks - 1).reshape(n_sub, n_col * col_cap)
    chosen = jnp.stack([chosen[1 - my_sub], chosen[my_sub]]).reshape(-1)
    outgoing = by_col.at[:, chosen].get(mode="promise_in_bounds")
    outgoing = outgoing.transpose(1, 0, 2).reshape(2, n_col, col_cap, rows_here, BLOCK)
    outgoing, corner, panel_send = lax.optimization_barrier((outgoing, corner, panel_send))
    lower, inverse = factor_corner(corner)
    pieces = [lax.dynamic_index_in_dim(panel_send, my_row, 0, keepdims=False)]
    for shift in range(1, n_row):
        piece = lax.dynamic_index_in_dim(panel_send, (my_row + shift) % n_row, 0, keepdims=False)
        pieces.append(lax.ppermute(piece, "row", [(i, (i + shift) % n_row) for i in range(n_row)]))
    panel_got = jnp.stack(pieces)
    panel_rows = None
    for which in range(n_sub):
        placement = receiving_table(
            row_map[which], my_row, row_blocks, front_row_blocks, row_cap, 0, n_row * row_cap
        )
        row_valid = placement < n_row * row_cap
        source = jnp.minimum(placement, n_row * row_cap - 1) // row_cap
        placement = ((my_row - source) % n_row) * row_cap + placement % row_cap
        got = panel_got[:, which].reshape(n_row * row_cap, panel_blocks, BLOCK, BLOCK)
        got = jnp.where(row_valid[:, None, None, None], got.at[placement].get(mode="promise_in_bounds"), 0.0)
        panel_rows = got if panel_rows is None else panel_rows + got
    panel_rows = panel_rows.transpose(0, 2, 1, 3).reshape(front_rows, PANEL)
    panel_rows = panel_rows + jnp.where(global_row[:, None] >= PANEL, coupling, 0.0)
    panel_rows = panel_rows + jnp.where(
        global_row[:, None] == jnp.arange(PANEL, dtype=jnp.int32)[None, :], full_diagonal[None, :PANEL], 0.0
    )
    other_half = lax.all_to_all(outgoing[0], "col", split_axis=0, concat_axis=0, tiled=True)
    other_half, lower, inverse = lax.optimization_barrier((other_half, lower, inverse))
    other_half = lax.ppermute(other_half, "sub", [(0, 1), (1, 0)])

    def row_sending(half, which):
        cols_of = lax.dynamic_index_in_dim(col_map, which, 0, keepdims=False)
        rows_of = lax.dynamic_index_in_dim(row_map, which, 0, keepdims=False)
        col_index = receiving_table(
            cols_of, my_group, col_blocks, front_col_blocks, col_cap, 0, n_col * col_cap
        )
        col_valid = col_index < n_col * col_cap
        col_index = jnp.minimum(col_index, n_col * col_cap - 1)
        row_index = sending_table(rows_of, my_row, row_blocks, front_row_blocks, n_row, row_cap)
        row_index = jnp.minimum(row_index, row_blocks - 1).reshape(n_row, row_cap)
        half = half.reshape(n_col * col_cap, row_blocks, BLOCK, BLOCK)
        sending = half.at[col_index[None, None, :], row_index[:, :, None]].get(
            mode="promise_in_bounds"
        )
        return sending, col_valid, rows_of

    def row_receiving(sending, col_valid, rows_of, by_permutes):
        placement = receiving_table(
            rows_of, my_row, row_blocks, front_row_blocks, row_cap, 0, n_row * row_cap
        )
        row_valid = placement < n_row * row_cap
        placement = jnp.minimum(placement, n_row * row_cap - 1)
        if by_permutes:
            pieces = [lax.dynamic_index_in_dim(sending, my_row, 0, keepdims=False)]
            for shift in range(1, n_row):
                piece = lax.dynamic_index_in_dim(sending, (my_row + shift) % n_row, 0, keepdims=False)
                pairs = [(i, (i + shift) % n_row) for i in range(n_row)]
                pieces.append(lax.ppermute(piece, "row", pairs))
            received = jnp.stack(pieces)
            source = placement // row_cap
            placement = ((my_row - source) % n_row) * row_cap + placement % row_cap
        else:
            received = lax.all_to_all(sending, "row", split_axis=0, concat_axis=0, tiled=True)
        received = received.reshape(n_row * row_cap, front_col_blocks, BLOCK, BLOCK)
        part = received.at[placement].get(mode="promise_in_bounds")
        keep = row_valid[:, None] & col_valid[None, :]
        return part, keep

    sending_other, col_valid_other, rows_other = row_sending(other_half, 1 - my_sub)
    sending_other, own_outgoing = lax.optimization_barrier((sending_other, outgoing[1]))
    part_other, keep_other = row_receiving(sending_other, col_valid_other, rows_other, True)
    own_half = lax.all_to_all(own_outgoing, "col", split_axis=0, concat_axis=0, tiled=True)
    own_half, part_other, panel_rows = lax.optimization_barrier((own_half, part_other, panel_rows))
    sending_own, col_valid_own, rows_own = row_sending(own_half, my_sub)
    part_own, keep_own = row_receiving(sending_own, col_valid_own, rows_own, False)
    assembled = jnp.where(keep_other[:, :, None, None], part_other, 0.0) + jnp.where(
        keep_own[:, :, None, None], part_own, 0.0
    )
    assembled = assembled.transpose(0, 2, 1, 3).reshape(front_rows, front_cols)

    global_col = my_group * front_cols + jnp.arange(front_cols, dtype=jnp.int32)
    on_diagonal = global_row[:, None] == global_col[None, :]
    assembled = assembled + jnp.where(on_diagonal, own_diagonal[None, :], 0.0)
    coupling_wide = jnp.concatenate(
        [coupling, jnp.zeros((front_rows, front_cols - PANEL), jnp.float32)], axis=1
    )
    coupling_mask = (global_row[:, None] >= PANEL) & (global_col[None, :] < PANEL)
    front_part = assembled + jnp.where(coupling_mask, coupling_wide, 0.0)
    theirs_start = my_group * front_cols % front_rows
    theirs_root = my_group * front_cols // front_rows
    own_rows = apply_inverse(panel_rows, inverse)
    top_rows = jnp.where(my_row == 0, lower, own_rows[:PANEL])
    own_rows = jnp.concatenate([top_rows, own_rows[PANEL:]], axis=0)
    theirs = lax.dynamic_slice_in_dim(own_rows, theirs_start, front_cols, 0)
    theirs = from_root(theirs, "row", theirs_root)
    update = lax.dot_general(
        own_rows, theirs, (((1,), (1,)), ((), ())), precision=lax.Precision.HIGHEST
    )
    panel_wide = jnp.concatenate(
        [own_rows, jnp.zeros((front_rows, front_cols - PANEL), jnp.float32)], axis=1
    )
    trailing = front_part - update
    result = jnp.where(
        global_col[None, :] < PANEL,
        panel_wide,
        jnp.where(global_row[:, None] < PANEL, 0.0, trailing),
    )
    return result


def solution(mesh):
    placed = (P("sub", "row", "col"), P(), P(), P(("sub", "col")), P("row", None))
    return jax.shard_map(
        shards, mesh=mesh, in_specs=placed, out_specs=P("row", ("sub", "col")), check_vma=False
    )
```

```python
import jax
import jax.numpy as jnp
from jax import lax
from jax.sharding import PartitionSpec as P

FRONT = 10240
PANEL = 512
BLOCK = 128


def from_root(value, axis, source):
    kept = jnp.where(lax.axis_index(axis) == source, value, 0).astype(value.dtype)
    return lax.psum(kept, axis)


def block_routes(parent_blocks, per_source, per_target):
    number = parent_blocks.shape[0]
    positions = jnp.arange(number, dtype=jnp.int32)
    source = positions // per_source
    target = parent_blocks // per_target
    earlier = (
        (source[:, None] == source[None, :])
        & (target[:, None] == target[None, :])
        & (positions[None, :] < positions[:, None])
    )
    slot_index = jnp.sum(earlier.astype(jnp.int32), axis=1)
    return (positions, source, target, slot_index, parent_blocks % per_target)


def sending_table(parent_blocks, own_index, per_source, per_target, targets, capacity):
    positions, source, target, slot_index, local_block = block_routes(
        parent_blocks, per_source, per_target
    )
    wanted = jnp.arange(targets * capacity, dtype=jnp.int32)
    matches = (source == own_index)[None, :] & (
        (target * capacity + slot_index)[None, :] == wanted[:, None]
    )
    within = positions % per_source
    return jnp.where(
        jnp.any(matches, axis=1),
        jnp.sum(jnp.where(matches, within[None, :], 0), axis=1),
        per_source,
    )


def receiving_table(parent_blocks, own_index, per_source, per_target, capacity, offset, empty_slot):
    positions, source, target, slot_index, local_block = block_routes(
        parent_blocks, per_source, per_target
    )
    wanted = jnp.arange(per_target, dtype=jnp.int32)
    matches = (target == own_index)[None, :] & (local_block[None, :] == wanted[:, None])
    flat_slot = (source + offset) * capacity + slot_index
    return jnp.where(
        jnp.any(matches, axis=1),
        jnp.sum(jnp.where(matches, flat_slot[None, :], 0), axis=1),
        empty_slot,
    )


def with_zero(blocks, axis):
    shape = list(blocks.shape)
    shape[axis] = 1
    return jnp.concatenate([blocks, jnp.zeros(shape, blocks.dtype)], axis=axis)


def symmetric_of(corner):
    return jnp.tril(corner) + jnp.tril(corner, -1).T


def factor_corner(corner):
    lower = jnp.linalg.cholesky(symmetric_of(corner))
    inverse = jax.scipy.linalg.solve_triangular(
        lower, jnp.eye(PANEL, dtype=jnp.float32), lower=True
    )
    return (lower, inverse)


def apply_inverse(rows, inverse):
    return lax.dot_general(rows, inverse, (((1,), (1,)), ((), ())), precision=lax.Precision.HIGHEST)


def early_corner(child_piece, row_map, col_map, full_diagonal):
    n_row = lax.axis_size("row")
    n_col = lax.axis_size("col")
    n_sub = lax.axis_size("sub")
    rows_here, cols_here = child_piece.shape
    row_blocks = rows_here // BLOCK
    col_blocks = cols_here // BLOCK
    panel_blocks = PANEL // BLOCK
    first_rows = min(row_blocks, -(-panel_blocks // n_row))
    first_cols = min(col_blocks, -(-panel_blocks // n_col))
    piece = child_piece[: first_rows * BLOCK, : first_cols * BLOCK]
    pieces = lax.all_gather(piece, ("sub", "row", "col"))
    pieces = pieces.reshape(n_sub, n_row, n_col, first_rows, BLOCK, first_cols, BLOCK)
    pieces = pieces.transpose(0, 1, 3, 2, 5, 4, 6).reshape(
        n_sub, n_row * first_rows, n_col * first_cols, BLOCK, BLOCK
    )
    row_pos = (
        jnp.arange(n_row, dtype=jnp.int32)[:, None] * row_blocks
        + jnp.arange(first_rows, dtype=jnp.int32)[None, :]
    ).reshape(-1)
    col_pos = (
        jnp.arange(n_col, dtype=jnp.int32)[:, None] * col_blocks
        + jnp.arange(first_cols, dtype=jnp.int32)[None, :]
    ).reshape(-1)
    corner = jnp.zeros((panel_blocks + 1, panel_blocks + 1, BLOCK, BLOCK), jnp.float32)
    for which in range(n_sub):
        rb = row_map[which][row_pos]
        cb = col_map[which][col_pos]
        rb = jnp.where(rb < panel_blocks, rb, panel_blocks)
        cb = jnp.where(cb < panel_blocks, cb, panel_blocks)
        corner = corner.at[rb[:, None], cb[None, :]].add(pieces[which])
    corner = corner[:panel_blocks, :panel_blocks].transpose(0, 2, 1, 3).reshape(PANEL, PANEL)
    return corner + jnp.diag(full_diagonal[:PANEL])


def shards(child, row_map, col_map, own_diagonal, coupling):
    n_row = lax.axis_size("row")
    n_col = lax.axis_size("col")
    n_group = lax.axis_size(("sub", "col"))
    my_row = lax.axis_index("row")
    my_col = lax.axis_index("col")
    my_sub = lax.axis_index("sub")
    my_group = lax.axis_index(("sub", "col"))
    child_piece = child[0]
    rows_here, cols_here = child_piece.shape
    front_rows = FRONT // n_row
    front_cols = FRONT // n_group
    row_blocks = rows_here // BLOCK
    col_blocks = cols_here // BLOCK
    front_row_blocks = front_rows // BLOCK
    front_col_blocks = front_cols // BLOCK
    row_cap = min(row_blocks, (front_row_blocks + n_row - 1) // n_row)
    col_cap = min(col_blocks, (front_col_blocks + n_col - 1) // n_col)
    n_sub = lax.axis_size("sub")
    my_rows_map = lax.dynamic_index_in_dim(row_map, my_sub, 0, keepdims=False)
    my_cols_map = lax.dynamic_index_in_dim(col_map, my_sub, 0, keepdims=False)

    full_diagonal = lax.all_gather(own_diagonal, ("sub", "col"), tiled=True)
    corner = early_corner(child_piece, row_map, col_map, full_diagonal)
    global_row = my_row * front_rows + jnp.arange(front_rows, dtype=jnp.int32)

    panel_blocks = PANEL // BLOCK
    first_cols = min(col_blocks, -(-panel_blocks // n_col))
    cands = lax.all_gather(child_piece[:, : first_cols * BLOCK], ("sub", "col"))
    cands = cands.reshape(n_sub, n_col, rows_here, first_cols, BLOCK).transpose(0, 1, 3, 2, 4)
    cands = cands.reshape(n_sub, n_col * first_cols, rows_here, BLOCK)
    cand_pos = (
        jnp.arange(n_col, dtype=jnp.int32)[:, None] * col_blocks
        + jnp.arange(first_cols, dtype=jnp.int32)[None, :]
    ).reshape(-1)
    panel_send = []
    for which in range(n_sub):
        found = col_map[which][cand_pos][None, :] == jnp.arange(panel_blocks, dtype=jnp.int32)[:, None]
        pick = jnp.argmax(found, axis=1)
        stored = jnp.where(jnp.any(found, axis=1)[:, None, None], cands[which][pick], 0.0)
        stored = stored.reshape(panel_blocks, row_blocks, BLOCK, BLOCK)
        pick_rows = sending_table(row_map[which], my_row, row_blocks, front_row_blocks, n_row, row_cap)
        pick_rows = jnp.minimum(pick_rows, row_blocks - 1).reshape(n_row, row_cap)
        panel_send.append(stored.at[:, pick_rows].get(mode="promise_in_bounds"))
    panel_send = jnp.stack(panel_send).transpose(2, 0, 3, 1, 4, 5)

    by_col = child_piece.reshape(rows_here, col_blocks, BLOCK)
    chosen = sending_table(my_cols_map, my_col, col_blocks, front_col_blocks, n_group, col_cap)
    chosen = jnp.minimum(chosen, col_blocks - 1).reshape(n_sub, n_col * col_cap)
    chosen = jnp.stack([chosen[1 - my_sub], chosen[my_sub]]).reshape(-1)
    outgoing = by_col.at[:, chosen].get(mode="promise_in_bounds")
    outgoing = outgoing.transpose(1, 0, 2).reshape(2, n_col, col_cap, rows_here, BLOCK)
    outgoing, corner = lax.optimization_barrier((outgoing, corner))
    lower, inverse = factor_corner(corner)
    other_half = lax.all_to_all(outgoing[0], "col", split_axis=0, concat_axis=0, tiled=True)
    other_half, lower, inverse, panel_send = lax.optimization_barrier(
        (other_half, lower, inverse, panel_send)
    )
    pieces = [lax.dynamic_index_in_dim(panel_send, my_row, 0, keepdims=False)]
    for shift in range(1, n_row):
        piece = lax.dynamic_index_in_dim(panel_send, (my_row + shift) % n_row, 0, keepdims=False)
        pieces.append(lax.ppermute(piece, "row", [(i, (i + shift) % n_row) for i in range(n_row)]))
    panel_got = jnp.stack(pieces)
    panel_rows = None
    for which in range(n_sub):
        placement = receiving_table(
            row_map[which], my_row, row_blocks, front_row_blocks, row_cap, 0, n_row * row_cap
        )
        row_valid = placement < n_row * row_cap
        source = jnp.minimum(placement, n_row * row_cap - 1) // row_cap
        placement = ((my_row - source) % n_row) * row_cap + placement % row_cap
        got = panel_got[:, which].reshape(n_row * row_cap, panel_blocks, BLOCK, BLOCK)
        got = jnp.where(row_valid[:, None, None, None], got.at[placement].get(mode="promise_in_bounds"), 0.0)
        panel_rows = got if panel_rows is None else panel_rows + got
    panel_rows = panel_rows.transpose(0, 2, 1, 3).reshape(front_rows, PANEL)
    panel_rows = panel_rows + jnp.where(global_row[:, None] >= PANEL, coupling, 0.0)
    panel_rows = panel_rows + jnp.where(
        global_row[:, None] == jnp.arange(PANEL, dtype=jnp.int32)[None, :], full_diagonal[None, :PANEL], 0.0
    )
    other_half = lax.ppermute(other_half, "sub", [(0, 1), (1, 0)])

    def row_sending(half, which):
        cols_of = lax.dynamic_index_in_dim(col_map, which, 0, keepdims=False)
        rows_of = lax.dynamic_index_in_dim(row_map, which, 0, keepdims=False)
        col_index = receiving_table(
            cols_of, my_group, col_blocks, front_col_blocks, col_cap, 0, n_col * col_cap
        )
        col_valid = col_index < n_col * col_cap
        col_index = jnp.minimum(col_index, n_col * col_cap - 1)
        row_index = sending_table(rows_of, my_row, row_blocks, front_row_blocks, n_row, row_cap)
        row_index = jnp.minimum(row_index, row_blocks - 1).reshape(n_row, row_cap)
        half = half.reshape(n_col * col_cap, row_blocks, BLOCK, BLOCK)
        sending = half.at[col_index[None, None, :], row_index[:, :, None]].get(
            mode="promise_in_bounds"
        )
        return sending, col_valid, rows_of

    def row_receiving(sending, col_valid, rows_of, by_permutes):
        placement = receiving_table(
            rows_of, my_row, row_blocks, front_row_blocks, row_cap, 0, n_row * row_cap
        )
        row_valid = placement < n_row * row_cap
        placement = jnp.minimum(placement, n_row * row_cap - 1)
        if by_permutes:
            pieces = [lax.dynamic_index_in_dim(sending, my_row, 0, keepdims=False)]
            for shift in range(1, n_row):
                piece = lax.dynamic_index_in_dim(sending, (my_row + shift) % n_row, 0, keepdims=False)
                pairs = [(i, (i + shift) % n_row) for i in range(n_row)]
                pieces.append(lax.ppermute(piece, "row", pairs))
            received = jnp.stack(pieces)
            source = placement // row_cap
            placement = ((my_row - source) % n_row) * row_cap + placement % row_cap
        else:
            received = lax.all_to_all(sending, "row", split_axis=0, concat_axis=0, tiled=True)
        received = received.reshape(n_row * row_cap, front_col_blocks, BLOCK, BLOCK)
        part = received.at[placement].get(mode="promise_in_bounds")
        keep = row_valid[:, None] & col_valid[None, :]
        return part, keep

    sending_other, col_valid_other, rows_other = row_sending(other_half, 1 - my_sub)
    sending_other, own_outgoing = lax.optimization_barrier((sending_other, outgoing[1]))
    part_other, keep_other = row_receiving(sending_other, col_valid_other, rows_other, True)
    own_half = lax.all_to_all(own_outgoing, "col", split_axis=0, concat_axis=0, tiled=True)
    own_half, part_other, panel_rows = lax.optimization_barrier((own_half, part_other, panel_rows))
    sending_own, col_valid_own, rows_own = row_sending(own_half, my_sub)
    part_own, keep_own = row_receiving(sending_own, col_valid_own, rows_own, False)
    assembled = jnp.where(keep_other[:, :, None, None], part_other, 0.0) + jnp.where(
        keep_own[:, :, None, None], part_own, 0.0
    )
    assembled = assembled.transpose(0, 2, 1, 3).reshape(front_rows, front_cols)

    global_col = my_group * front_cols + jnp.arange(front_cols, dtype=jnp.int32)
    on_diagonal = global_row[:, None] == global_col[None, :]
    assembled = assembled + jnp.where(on_diagonal, own_diagonal[None, :], 0.0)
    coupling_wide = jnp.concatenate(
        [coupling, jnp.zeros((front_rows, front_cols - PANEL), jnp.float32)], axis=1
    )
    coupling_mask = (global_row[:, None] >= PANEL) & (global_col[None, :] < PANEL)
    front_part = assembled + jnp.where(coupling_mask, coupling_wide, 0.0)
    theirs_start = my_group * front_cols % front_rows
    theirs_root = my_group * front_cols // front_rows
    own_rows = apply_inverse(panel_rows, inverse)
    top_rows = jnp.where(my_row == 0, lower, own_rows[:PANEL])
    own_rows = jnp.concatenate([top_rows, own_rows[PANEL:]], axis=0)
    theirs = lax.dynamic_slice_in_dim(own_rows, theirs_start, front_cols, 0)
    theirs = from_root(theirs, "row", theirs_root)
    update = lax.dot_general(
        own_rows, theirs, (((1,), (1,)), ((), ())), precision=lax.Precision.HIGHEST
    )
    panel_wide = jnp.concatenate(
        [own_rows, jnp.zeros((front_rows, front_cols - PANEL), jnp.float32)], axis=1
    )
    trailing = front_part - update
    result = jnp.where(
        global_col[None, :] < PANEL,
        panel_wide,
        jnp.where(global_row[:, None] < PANEL, 0.0, trailing),
    )
    return result


def solution(mesh):
    placed = (P("sub", "row", "col"), P(), P(), P(("sub", "col")), P("row", None))
    return jax.shard_map(
        shards, mesh=mesh, in_specs=placed, out_specs=P("row", ("sub", "col")), check_vma=False
    )
```

```python
import jax
import jax.numpy as jnp
from jax import lax
from jax.sharding import PartitionSpec as P

FRONT = 10240
PANEL = 512
BLOCK = 128


def from_root(value, axis, source):
    kept = jnp.where(lax.axis_index(axis) == source, value, 0).astype(value.dtype)
    return lax.psum(kept, axis)


def block_routes(parent_blocks, per_source, per_target):
    number = parent_blocks.shape[0]
    positions = jnp.arange(number, dtype=jnp.int32)
    source = positions // per_source
    target = parent_blocks // per_target
    earlier = (
        (source[:, None] == source[None, :])
        & (target[:, None] == target[None, :])
        & (positions[None, :] < positions[:, None])
    )
    slot_index = jnp.sum(earlier.astype(jnp.int32), axis=1)
    return (positions, source, target, slot_index, parent_blocks % per_target)


def sending_table(parent_blocks, own_index, per_source, per_target, targets, capacity):
    positions, source, target, slot_index, local_block = block_routes(
        parent_blocks, per_source, per_target
    )
    wanted = jnp.arange(targets * capacity, dtype=jnp.int32)
    matches = (source == own_index)[None, :] & (
        (target * capacity + slot_index)[None, :] == wanted[:, None]
    )
    within = positions % per_source
    return jnp.where(
        jnp.any(matches, axis=1),
        jnp.sum(jnp.where(matches, within[None, :], 0), axis=1),
        per_source,
    )


def receiving_table(parent_blocks, own_index, per_source, per_target, capacity, offset, empty_slot):
    positions, source, target, slot_index, local_block = block_routes(
        parent_blocks, per_source, per_target
    )
    wanted = jnp.arange(per_target, dtype=jnp.int32)
    matches = (target == own_index)[None, :] & (local_block[None, :] == wanted[:, None])
    flat_slot = (source + offset) * capacity + slot_index
    return jnp.where(
        jnp.any(matches, axis=1),
        jnp.sum(jnp.where(matches, flat_slot[None, :], 0), axis=1),
        empty_slot,
    )


def with_zero(blocks, axis):
    shape = list(blocks.shape)
    shape[axis] = 1
    return jnp.concatenate([blocks, jnp.zeros(shape, blocks.dtype)], axis=axis)


def symmetric_of(corner):
    return jnp.tril(corner) + jnp.tril(corner, -1).T


def factor_corner(corner):
    lower = jnp.linalg.cholesky(symmetric_of(corner))
    inverse = jax.scipy.linalg.solve_triangular(
        lower, jnp.eye(PANEL, dtype=jnp.float32), lower=True
    )
    return (lower, inverse)


def apply_inverse(rows, inverse):
    return lax.dot_general(rows, inverse, (((1,), (1,)), ((), ())), precision=lax.Precision.HIGHEST)


def early_corner(child_piece, row_map, col_map, full_diagonal):
    n_row = lax.axis_size("row")
    n_col = lax.axis_size("col")
    n_sub = lax.axis_size("sub")
    rows_here, cols_here = child_piece.shape
    row_blocks = rows_here // BLOCK
    col_blocks = cols_here // BLOCK
    panel_blocks = PANEL // BLOCK
    first_rows = min(row_blocks, -(-panel_blocks // n_row))
    first_cols = min(col_blocks, -(-panel_blocks // n_col))
    piece = child_piece[: first_rows * BLOCK, : first_cols * BLOCK]
    pieces = lax.all_gather(piece, ("sub", "row", "col"))
    pieces = pieces.reshape(n_sub, n_row, n_col, first_rows, BLOCK, first_cols, BLOCK)
    pieces = pieces.transpose(0, 1, 3, 2, 5, 4, 6).reshape(
        n_sub, n_row * first_rows, n_col * first_cols, BLOCK, BLOCK
    )
    row_pos = (
        jnp.arange(n_row, dtype=jnp.int32)[:, None] * row_blocks
        + jnp.arange(first_rows, dtype=jnp.int32)[None, :]
    ).reshape(-1)
    col_pos = (
        jnp.arange(n_col, dtype=jnp.int32)[:, None] * col_blocks
        + jnp.arange(first_cols, dtype=jnp.int32)[None, :]
    ).reshape(-1)
    corner = jnp.zeros((panel_blocks + 1, panel_blocks + 1, BLOCK, BLOCK), jnp.float32)
    for which in range(n_sub):
        rb = row_map[which][row_pos]
        cb = col_map[which][col_pos]
        rb = jnp.where(rb < panel_blocks, rb, panel_blocks)
        cb = jnp.where(cb < panel_blocks, cb, panel_blocks)
        corner = corner.at[rb[:, None], cb[None, :]].add(pieces[which])
    corner = corner[:panel_blocks, :panel_blocks].transpose(0, 2, 1, 3).reshape(PANEL, PANEL)
    return corner + jnp.diag(full_diagonal[:PANEL])


def shards(child, row_map, col_map, own_diagonal, coupling):
    n_row = lax.axis_size("row")
    n_col = lax.axis_size("col")
    n_group = lax.axis_size(("sub", "col"))
    my_row = lax.axis_index("row")
    my_col = lax.axis_index("col")
    my_sub = lax.axis_index("sub")
    my_group = lax.axis_index(("sub", "col"))
    child_piece = child[0]
    rows_here, cols_here = child_piece.shape
    front_rows = FRONT // n_row
    front_cols = FRONT // n_group
    row_blocks = rows_here // BLOCK
    col_blocks = cols_here // BLOCK
    front_row_blocks = front_rows // BLOCK
    front_col_blocks = front_cols // BLOCK
    row_cap = min(row_blocks, (front_row_blocks + n_row - 1) // n_row)
    col_cap = min(col_blocks, (front_col_blocks + n_col - 1) // n_col)
    n_sub = lax.axis_size("sub")
    my_rows_map = lax.dynamic_index_in_dim(row_map, my_sub, 0, keepdims=False)
    my_cols_map = lax.dynamic_index_in_dim(col_map, my_sub, 0, keepdims=False)

    full_diagonal = lax.all_gather(own_diagonal, ("sub", "col"), tiled=True)
    corner = early_corner(child_piece, row_map, col_map, full_diagonal)
    global_row = my_row * front_rows + jnp.arange(front_rows, dtype=jnp.int32)

    panel_blocks = PANEL // BLOCK
    first_cols = min(col_blocks, -(-panel_blocks // n_col))
    cands = lax.all_gather(child_piece[:, : first_cols * BLOCK], "col")
    cands = jnp.stack([cands, lax.ppermute(cands, "sub", [(0, 1), (1, 0)])])
    cands = cands.reshape(n_sub, n_col, rows_here, first_cols, BLOCK).transpose(0, 1, 3, 2, 4)
    cands = cands.reshape(n_sub, n_col * first_cols, rows_here, BLOCK)
    cand_pos = (
        jnp.arange(n_col, dtype=jnp.int32)[:, None] * col_blocks
        + jnp.arange(first_cols, dtype=jnp.int32)[None, :]
    ).reshape(-1)
    panel_send = []
    for which in range(n_sub):
        found = col_map[which][cand_pos][None, :] == jnp.arange(panel_blocks, dtype=jnp.int32)[:, None]
        pick = jnp.argmax(found, axis=1)
        mine = lax.dynamic_index_in_dim(cands, (which + my_sub) % n_sub, 0, keepdims=False)
        stored = jnp.where(jnp.any(found, axis=1)[:, None, None], mine[pick], 0.0)
        stored = stored.reshape(panel_blocks, row_blocks, BLOCK, BLOCK)
        pick_rows = sending_table(row_map[which], my_row, row_blocks, front_row_blocks, n_row, row_cap)
        pick_rows = jnp.minimum(pick_rows, row_blocks - 1).reshape(n_row, row_cap)
        panel_send.append(stored.at[:, pick_rows].get(mode="promise_in_bounds"))
    panel_send = jnp.stack(panel_send).transpose(2, 0, 3, 1, 4, 5)

    by_col = child_piece.reshape(rows_here, col_blocks, BLOCK)
    chosen = sending_table(my_cols_map, my_col, col_blocks, front_col_blocks, n_group, col_cap)
    chosen = jnp.minimum(chosen, col_blocks - 1).reshape(n_sub, n_col * col_cap)
    chosen = jnp.stack([chosen[1 - my_sub], chosen[my_sub]]).reshape(-1)
    outgoing = by_col.at[:, chosen].get(mode="promise_in_bounds")
    outgoing = outgoing.transpose(1, 0, 2).reshape(2, n_col, col_cap, rows_here, BLOCK)
    outgoing, corner = lax.optimization_barrier((outgoing, corner))
    lower, inverse = factor_corner(corner)
    other_half = lax.all_to_all(outgoing[0], "col", split_axis=0, concat_axis=0, tiled=True)
    other_half, lower, inverse, panel_send = lax.optimization_barrier(
        (other_half, lower, inverse, panel_send)
    )
    pieces = [lax.dynamic_index_in_dim(panel_send, my_row, 0, keepdims=False)]
    for shift in range(1, n_row):
        piece = lax.dynamic_index_in_dim(panel_send, (my_row + shift) % n_row, 0, keepdims=False)
        pieces.append(lax.ppermute(piece, "row", [(i, (i + shift) % n_row) for i in range(n_row)]))
    panel_got = jnp.stack(pieces)
    panel_rows = None
    for which in range(n_sub):
        placement = receiving_table(
            row_map[which], my_row, row_blocks, front_row_blocks, row_cap, 0, n_row * row_cap
        )
        row_valid = placement < n_row * row_cap
        source = jnp.minimum(placement, n_row * row_cap - 1) // row_cap
        placement = ((my_row - source) % n_row) * row_cap + placement % row_cap
        got = panel_got[:, which].reshape(n_row * row_cap, panel_blocks, BLOCK, BLOCK)
        got = jnp.where(row_valid[:, None, None, None], got.at[placement].get(mode="promise_in_bounds"), 0.0)
        panel_rows = got if panel_rows is None else panel_rows + got
    panel_rows = panel_rows.transpose(0, 2, 1, 3).reshape(front_rows, PANEL)
    panel_rows = panel_rows + jnp.where(global_row[:, None] >= PANEL, coupling, 0.0)
    panel_rows = panel_rows + jnp.where(
        global_row[:, None] == jnp.arange(PANEL, dtype=jnp.int32)[None, :], full_diagonal[None, :PANEL], 0.0
    )
    other_half = lax.ppermute(other_half, "sub", [(0, 1), (1, 0)])

    def row_sending(half, which):
        cols_of = lax.dynamic_index_in_dim(col_map, which, 0, keepdims=False)
        rows_of = lax.dynamic_index_in_dim(row_map, which, 0, keepdims=False)
        col_index = receiving_table(
            cols_of, my_group, col_blocks, front_col_blocks, col_cap, 0, n_col * col_cap
        )
        col_valid = col_index < n_col * col_cap
        col_index = jnp.minimum(col_index, n_col * col_cap - 1)
        row_index = sending_table(rows_of, my_row, row_blocks, front_row_blocks, n_row, row_cap)
        row_index = jnp.minimum(row_index, row_blocks - 1).reshape(n_row, row_cap)
        half = half.reshape(n_col * col_cap, row_blocks, BLOCK, BLOCK)
        sending = half.at[col_index[None, None, :], row_index[:, :, None]].get(
            mode="promise_in_bounds"
        )
        return sending, col_valid, rows_of

    def row_receiving(sending, col_valid, rows_of, by_permutes):
        placement = receiving_table(
            rows_of, my_row, row_blocks, front_row_blocks, row_cap, 0, n_row * row_cap
        )
        row_valid = placement < n_row * row_cap
        placement = jnp.minimum(placement, n_row * row_cap - 1)
        if by_permutes:
            pieces = [lax.dynamic_index_in_dim(sending, my_row, 0, keepdims=False)]
            for shift in range(1, n_row):
                piece = lax.dynamic_index_in_dim(sending, (my_row + shift) % n_row, 0, keepdims=False)
                pairs = [(i, (i + shift) % n_row) for i in range(n_row)]
                pieces.append(lax.ppermute(piece, "row", pairs))
            received = jnp.stack(pieces)
            source = placement // row_cap
            placement = ((my_row - source) % n_row) * row_cap + placement % row_cap
        else:
            received = lax.all_to_all(sending, "row", split_axis=0, concat_axis=0, tiled=True)
        received = received.reshape(n_row * row_cap, front_col_blocks, BLOCK, BLOCK)
        part = received.at[placement].get(mode="promise_in_bounds")
        keep = row_valid[:, None] & col_valid[None, :]
        return part, keep

    sending_other, col_valid_other, rows_other = row_sending(other_half, 1 - my_sub)
    sending_other, own_outgoing = lax.optimization_barrier((sending_other, outgoing[1]))
    part_other, keep_other = row_receiving(sending_other, col_valid_other, rows_other, True)
    own_half = lax.all_to_all(own_outgoing, "col", split_axis=0, concat_axis=0, tiled=True)
    own_half, part_other, panel_rows = lax.optimization_barrier((own_half, part_other, panel_rows))
    sending_own, col_valid_own, rows_own = row_sending(own_half, my_sub)
    part_own, keep_own = row_receiving(sending_own, col_valid_own, rows_own, False)
    assembled = jnp.where(keep_other[:, :, None, None], part_other, 0.0) + jnp.where(
        keep_own[:, :, None, None], part_own, 0.0
    )
    assembled = assembled.transpose(0, 2, 1, 3).reshape(front_rows, front_cols)

    global_col = my_group * front_cols + jnp.arange(front_cols, dtype=jnp.int32)
    on_diagonal = global_row[:, None] == global_col[None, :]
    assembled = assembled + jnp.where(on_diagonal, own_diagonal[None, :], 0.0)
    coupling_wide = jnp.concatenate(
        [coupling, jnp.zeros((front_rows, front_cols - PANEL), jnp.float32)], axis=1
    )
    coupling_mask = (global_row[:, None] >= PANEL) & (global_col[None, :] < PANEL)
    front_part = assembled + jnp.where(coupling_mask, coupling_wide, 0.0)
    theirs_start = my_group * front_cols % front_rows
    theirs_root = my_group * front_cols // front_rows
    own_rows = apply_inverse(panel_rows, inverse)
    top_rows = jnp.where(my_row == 0, lower, own_rows[:PANEL])
    own_rows = jnp.concatenate([top_rows, own_rows[PANEL:]], axis=0)
    theirs = lax.dynamic_slice_in_dim(own_rows, theirs_start, front_cols, 0)
    theirs = from_root(theirs, "row", theirs_root)
    update = lax.dot_general(
        own_rows, theirs, (((1,), (1,)), ((), ())), precision=lax.Precision.HIGHEST
    )
    panel_wide = jnp.concatenate(
        [own_rows, jnp.zeros((front_rows, front_cols - PANEL), jnp.float32)], axis=1
    )
    trailing = front_part - update
    result = jnp.where(
        global_col[None, :] < PANEL,
        panel_wide,
        jnp.where(global_row[:, None] < PANEL, 0.0, trailing),
    )
    return result


def solution(mesh):
    placed = (P("sub", "row", "col"), P(), P(), P(("sub", "col")), P("row", None))
    return jax.shard_map(
        shards, mesh=mesh, in_specs=placed, out_specs=P("row", ("sub", "col")), check_vma=False
    )
```

```python
import jax
import jax.numpy as jnp
from jax import lax
from jax.sharding import PartitionSpec as P

FRONT = 10240
PANEL = 512
BLOCK = 128


def from_root(value, axis, source):
    kept = jnp.where(lax.axis_index(axis) == source, value, 0).astype(value.dtype)
    return lax.psum(kept, axis)


def block_routes(parent_blocks, per_source, per_target):
    number = parent_blocks.shape[0]
    positions = jnp.arange(number, dtype=jnp.int32)
    source = positions // per_source
    target = parent_blocks // per_target
    earlier = (
        (source[:, None] == source[None, :])
        & (target[:, None] == target[None, :])
        & (positions[None, :] < positions[:, None])
    )
    slot_index = jnp.sum(earlier.astype(jnp.int32), axis=1)
    return (positions, source, target, slot_index, parent_blocks % per_target)


def sending_table(parent_blocks, own_index, per_source, per_target, targets, capacity):
    positions, source, target, slot_index, local_block = block_routes(
        parent_blocks, per_source, per_target
    )
    wanted = jnp.arange(targets * capacity, dtype=jnp.int32)
    matches = (source == own_index)[None, :] & (
        (target * capacity + slot_index)[None, :] == wanted[:, None]
    )
    within = positions % per_source
    return jnp.where(
        jnp.any(matches, axis=1),
        jnp.sum(jnp.where(matches, within[None, :], 0), axis=1),
        per_source,
    )


def receiving_table(parent_blocks, own_index, per_source, per_target, capacity, offset, empty_slot):
    positions, source, target, slot_index, local_block = block_routes(
        parent_blocks, per_source, per_target
    )
    wanted = jnp.arange(per_target, dtype=jnp.int32)
    matches = (target == own_index)[None, :] & (local_block[None, :] == wanted[:, None])
    flat_slot = (source + offset) * capacity + slot_index
    return jnp.where(
        jnp.any(matches, axis=1),
        jnp.sum(jnp.where(matches, flat_slot[None, :], 0), axis=1),
        empty_slot,
    )


def with_zero(blocks, axis):
    shape = list(blocks.shape)
    shape[axis] = 1
    return jnp.concatenate([blocks, jnp.zeros(shape, blocks.dtype)], axis=axis)


def symmetric_of(corner):
    return jnp.tril(corner) + jnp.tril(corner, -1).T


def factor_corner(corner):
    lower = jnp.linalg.cholesky(symmetric_of(corner))
    inverse = jax.scipy.linalg.solve_triangular(
        lower, jnp.eye(PANEL, dtype=jnp.float32), lower=True
    )
    return (lower, inverse)


def apply_inverse(rows, inverse):
    return lax.dot_general(rows, inverse, (((1,), (1,)), ((), ())), precision=lax.Precision.HIGHEST)


def early_corner(child_piece, row_map, col_map, full_diagonal):
    n_row = lax.axis_size("row")
    n_col = lax.axis_size("col")
    n_sub = lax.axis_size("sub")
    rows_here, cols_here = child_piece.shape
    row_blocks = rows_here // BLOCK
    col_blocks = cols_here // BLOCK
    panel_blocks = PANEL // BLOCK
    first_rows = min(row_blocks, -(-panel_blocks // n_row))
    first_cols = min(col_blocks, -(-panel_blocks // n_col))
    piece = child_piece[: first_rows * BLOCK, : first_cols * BLOCK]
    pieces = lax.all_gather(piece, ("sub", "row", "col"))
    pieces = pieces.reshape(n_sub, n_row, n_col, first_rows, BLOCK, first_cols, BLOCK)
    pieces = pieces.transpose(0, 1, 3, 2, 5, 4, 6).reshape(
        n_sub, n_row * first_rows, n_col * first_cols, BLOCK, BLOCK
    )
    row_pos = (
        jnp.arange(n_row, dtype=jnp.int32)[:, None] * row_blocks
        + jnp.arange(first_rows, dtype=jnp.int32)[None, :]
    ).reshape(-1)
    col_pos = (
        jnp.arange(n_col, dtype=jnp.int32)[:, None] * col_blocks
        + jnp.arange(first_cols, dtype=jnp.int32)[None, :]
    ).reshape(-1)
    corner = jnp.zeros((panel_blocks + 1, panel_blocks + 1, BLOCK, BLOCK), jnp.float32)
    for which in range(n_sub):
        rb = row_map[which][row_pos]
        cb = col_map[which][col_pos]
        rb = jnp.where(rb < panel_blocks, rb, panel_blocks)
        cb = jnp.where(cb < panel_blocks, cb, panel_blocks)
        corner = corner.at[rb[:, None], cb[None, :]].add(pieces[which])
    corner = corner[:panel_blocks, :panel_blocks].transpose(0, 2, 1, 3).reshape(PANEL, PANEL)
    return corner + jnp.diag(full_diagonal[:PANEL])


def shards(child, row_map, col_map, own_diagonal, coupling):
    n_row = lax.axis_size("row")
    n_col = lax.axis_size("col")
    n_group = lax.axis_size(("sub", "col"))
    my_row = lax.axis_index("row")
    my_col = lax.axis_index("col")
    my_sub = lax.axis_index("sub")
    my_group = lax.axis_index(("sub", "col"))
    child_piece = child[0]
    rows_here, cols_here = child_piece.shape
    front_rows = FRONT // n_row
    front_cols = FRONT // n_group
    row_blocks = rows_here // BLOCK
    col_blocks = cols_here // BLOCK
    front_row_blocks = front_rows // BLOCK
    front_col_blocks = front_cols // BLOCK
    row_cap = min(row_blocks, (front_row_blocks + n_row - 1) // n_row)
    col_cap = min(col_blocks, (front_col_blocks + n_col - 1) // n_col)
    n_sub = lax.axis_size("sub")
    my_rows_map = lax.dynamic_index_in_dim(row_map, my_sub, 0, keepdims=False)
    my_cols_map = lax.dynamic_index_in_dim(col_map, my_sub, 0, keepdims=False)

    full_diagonal = lax.all_gather(own_diagonal, ("sub", "col"), tiled=True)
    corner = early_corner(child_piece, row_map, col_map, full_diagonal)
    global_row = my_row * front_rows + jnp.arange(front_rows, dtype=jnp.int32)

    panel_blocks = PANEL // BLOCK
    first_cols = min(col_blocks, -(-panel_blocks // n_col))
    own_cands = child_piece[:, : first_cols * BLOCK].reshape(row_blocks, BLOCK, first_cols * BLOCK)
    pick_rows = sending_table(my_rows_map, my_row, row_blocks, front_row_blocks, n_row, row_cap)
    pick_rows = jnp.minimum(pick_rows, row_blocks - 1).reshape(n_row, row_cap)
    cand_send = own_cands.at[pick_rows].get(mode="promise_in_bounds")
    pieces = [lax.dynamic_index_in_dim(cand_send, my_row, 0, keepdims=False)]
    for shift in range(1, n_row):
        piece = lax.dynamic_index_in_dim(cand_send, (my_row + shift) % n_row, 0, keepdims=False)
        pieces.append(lax.ppermute(piece, "row", [(i, (i + shift) % n_row) for i in range(n_row)]))
    cand_got = jnp.stack(pieces).reshape(n_row * row_cap, BLOCK, first_cols * BLOCK)
    placement = receiving_table(
        my_rows_map, my_row, row_blocks, front_row_blocks, row_cap, 0, n_row * row_cap
    )
    row_valid = placement < n_row * row_cap
    source = jnp.minimum(placement, n_row * row_cap - 1) // row_cap
    placement = ((my_row - source) % n_row) * row_cap + placement % row_cap
    cand_rows = jnp.where(
        row_valid[:, None, None], cand_got.at[placement].get(mode="promise_in_bounds"), 0.0
    )
    cands = lax.all_gather(cand_rows, "col")
    cands = jnp.stack([cands, lax.ppermute(cands, "sub", [(0, 1), (1, 0)])])
    cands = cands.reshape(n_sub, n_col, front_row_blocks, BLOCK, first_cols, BLOCK)
    cands = cands.transpose(0, 1, 4, 2, 3, 5).reshape(
        n_sub, n_col * first_cols, front_row_blocks, BLOCK, BLOCK
    )
    cand_pos = (
        jnp.arange(n_col, dtype=jnp.int32)[:, None] * col_blocks
        + jnp.arange(first_cols, dtype=jnp.int32)[None, :]
    ).reshape(-1)
    panel_rows = None
    for which in range(n_sub):
        found = col_map[which][cand_pos][None, :] == jnp.arange(panel_blocks, dtype=jnp.int32)[:, None]
        pick = jnp.argmax(found, axis=1)
        mine = lax.dynamic_index_in_dim(cands, (which + my_sub) % n_sub, 0, keepdims=False)
        got = jnp.where(jnp.any(found, axis=1)[:, None, None, None], mine[pick], 0.0)
        panel_rows = got if panel_rows is None else panel_rows + got
    panel_rows = panel_rows.transpose(1, 2, 0, 3).reshape(front_rows, PANEL)
    panel_rows = panel_rows + jnp.where(global_row[:, None] >= PANEL, coupling, 0.0)
    panel_rows = panel_rows + jnp.where(
        global_row[:, None] == jnp.arange(PANEL, dtype=jnp.int32)[None, :], full_diagonal[None, :PANEL], 0.0
    )

    by_col = child_piece.reshape(rows_here, col_blocks, BLOCK)
    chosen = sending_table(my_cols_map, my_col, col_blocks, front_col_blocks, n_group, col_cap)
    chosen = jnp.minimum(chosen, col_blocks - 1).reshape(n_sub, n_col * col_cap)
    chosen = jnp.stack([chosen[1 - my_sub], chosen[my_sub]]).reshape(-1)
    outgoing = by_col.at[:, chosen].get(mode="promise_in_bounds")
    outgoing = outgoing.transpose(1, 0, 2).reshape(2, n_col, col_cap, rows_here, BLOCK)
    outgoing, corner = lax.optimization_barrier((outgoing, corner))
    lower, inverse = factor_corner(corner)
    other_half = lax.all_to_all(outgoing[0], "col", split_axis=0, concat_axis=0, tiled=True)
    other_half, lower, inverse, panel_rows = lax.optimization_barrier(
        (other_half, lower, inverse, panel_rows)
    )
    other_half = lax.ppermute(other_half, "sub", [(0, 1), (1, 0)])

    def row_sending(half, which):
        cols_of = lax.dynamic_index_in_dim(col_map, which, 0, keepdims=False)
        rows_of = lax.dynamic_index_in_dim(row_map, which, 0, keepdims=False)
        col_index = receiving_table(
            cols_of, my_group, col_blocks, front_col_blocks, col_cap, 0, n_col * col_cap
        )
        col_valid = col_index < n_col * col_cap
        col_index = jnp.minimum(col_index, n_col * col_cap - 1)
        row_index = sending_table(rows_of, my_row, row_blocks, front_row_blocks, n_row, row_cap)
        row_index = jnp.minimum(row_index, row_blocks - 1).reshape(n_row, row_cap)
        half = half.reshape(n_col * col_cap, row_blocks, BLOCK, BLOCK)
        sending = half.at[col_index[None, None, :], row_index[:, :, None]].get(
            mode="promise_in_bounds"
        )
        return sending, col_valid, rows_of

    def row_receiving(sending, col_valid, rows_of, by_permutes):
        placement = receiving_table(
            rows_of, my_row, row_blocks, front_row_blocks, row_cap, 0, n_row * row_cap
        )
        row_valid = placement < n_row * row_cap
        placement = jnp.minimum(placement, n_row * row_cap - 1)
        if by_permutes:
            pieces = [lax.dynamic_index_in_dim(sending, my_row, 0, keepdims=False)]
            for shift in range(1, n_row):
                piece = lax.dynamic_index_in_dim(sending, (my_row + shift) % n_row, 0, keepdims=False)
                pairs = [(i, (i + shift) % n_row) for i in range(n_row)]
                pieces.append(lax.ppermute(piece, "row", pairs))
            received = jnp.stack(pieces)
            source = placement // row_cap
            placement = ((my_row - source) % n_row) * row_cap + placement % row_cap
        else:
            received = lax.all_to_all(sending, "row", split_axis=0, concat_axis=0, tiled=True)
        received = received.reshape(n_row * row_cap, front_col_blocks, BLOCK, BLOCK)
        part = received.at[placement].get(mode="promise_in_bounds")
        keep = row_valid[:, None] & col_valid[None, :]
        return part, keep

    sending_other, col_valid_other, rows_other = row_sending(other_half, 1 - my_sub)
    sending_other, own_outgoing = lax.optimization_barrier((sending_other, outgoing[1]))
    part_other, keep_other = row_receiving(sending_other, col_valid_other, rows_other, True)
    own_half = lax.all_to_all(own_outgoing, "col", split_axis=0, concat_axis=0, tiled=True)
    own_half, part_other = lax.optimization_barrier((own_half, part_other))
    sending_own, col_valid_own, rows_own = row_sending(own_half, my_sub)
    part_own, keep_own = row_receiving(sending_own, col_valid_own, rows_own, False)
    assembled = jnp.where(keep_other[:, :, None, None], part_other, 0.0) + jnp.where(
        keep_own[:, :, None, None], part_own, 0.0
    )
    assembled = assembled.transpose(0, 2, 1, 3).reshape(front_rows, front_cols)

    global_col = my_group * front_cols + jnp.arange(front_cols, dtype=jnp.int32)
    on_diagonal = global_row[:, None] == global_col[None, :]
    assembled = assembled + jnp.where(on_diagonal, own_diagonal[None, :], 0.0)
    coupling_wide = jnp.concatenate(
        [coupling, jnp.zeros((front_rows, front_cols - PANEL), jnp.float32)], axis=1
    )
    coupling_mask = (global_row[:, None] >= PANEL) & (global_col[None, :] < PANEL)
    front_part = assembled + jnp.where(coupling_mask, coupling_wide, 0.0)
    theirs_start = my_group * front_cols % front_rows
    theirs_root = my_group * front_cols // front_rows
    own_rows = apply_inverse(panel_rows, inverse)
    top_rows = jnp.where(my_row == 0, lower, own_rows[:PANEL])
    own_rows = jnp.concatenate([top_rows, own_rows[PANEL:]], axis=0)
    theirs = lax.dynamic_slice_in_dim(own_rows, theirs_start, front_cols, 0)
    theirs = from_root(theirs, "row", theirs_root)
    update = lax.dot_general(
        own_rows, theirs, (((1,), (1,)), ((), ())), precision=lax.Precision.HIGHEST
    )
    panel_wide = jnp.concatenate(
        [own_rows, jnp.zeros((front_rows, front_cols - PANEL), jnp.float32)], axis=1
    )
    trailing = front_part - update
    result = jnp.where(
        global_col[None, :] < PANEL,
        panel_wide,
        jnp.where(global_row[:, None] < PANEL, 0.0, trailing),
    )
    return result


def solution(mesh):
    placed = (P("sub", "row", "col"), P(), P(), P(("sub", "col")), P("row", None))
    return jax.shard_map(
        shards, mesh=mesh, in_specs=placed, out_specs=P("row", ("sub", "col")), check_vma=False
    )
```

```python
import jax
import jax.numpy as jnp
from jax import lax
from jax.sharding import PartitionSpec as P

FRONT = 10240
PANEL = 512
BLOCK = 128


def from_root(value, axis, source):
    kept = jnp.where(lax.axis_index(axis) == source, value, 0).astype(value.dtype)
    return lax.psum(kept, axis)


def block_routes(parent_blocks, per_source, per_target):
    number = parent_blocks.shape[0]
    positions = jnp.arange(number, dtype=jnp.int32)
    source = positions // per_source
    target = parent_blocks // per_target
    earlier = (
        (source[:, None] == source[None, :])
        & (target[:, None] == target[None, :])
        & (positions[None, :] < positions[:, None])
    )
    slot_index = jnp.sum(earlier.astype(jnp.int32), axis=1)
    return (positions, source, target, slot_index, parent_blocks % per_target)


def sending_table(parent_blocks, own_index, per_source, per_target, targets, capacity):
    positions, source, target, slot_index, local_block = block_routes(
        parent_blocks, per_source, per_target
    )
    wanted = jnp.arange(targets * capacity, dtype=jnp.int32)
    matches = (source == own_index)[None, :] & (
        (target * capacity + slot_index)[None, :] == wanted[:, None]
    )
    within = positions % per_source
    return jnp.where(
        jnp.any(matches, axis=1),
        jnp.sum(jnp.where(matches, within[None, :], 0), axis=1),
        per_source,
    )


def receiving_table(parent_blocks, own_index, per_source, per_target, capacity, offset, empty_slot):
    positions, source, target, slot_index, local_block = block_routes(
        parent_blocks, per_source, per_target
    )
    wanted = jnp.arange(per_target, dtype=jnp.int32)
    matches = (target == own_index)[None, :] & (local_block[None, :] == wanted[:, None])
    flat_slot = (source + offset) * capacity + slot_index
    return jnp.where(
        jnp.any(matches, axis=1),
        jnp.sum(jnp.where(matches, flat_slot[None, :], 0), axis=1),
        empty_slot,
    )


def with_zero(blocks, axis):
    shape = list(blocks.shape)
    shape[axis] = 1
    return jnp.concatenate([blocks, jnp.zeros(shape, blocks.dtype)], axis=axis)


def symmetric_of(corner):
    return jnp.tril(corner) + jnp.tril(corner, -1).T


def factor_corner(corner):
    lower = jnp.linalg.cholesky(symmetric_of(corner))
    inverse = jax.scipy.linalg.solve_triangular(
        lower, jnp.eye(PANEL, dtype=jnp.float32), lower=True
    )
    return (lower, inverse)


def apply_inverse(rows, inverse):
    return lax.dot_general(rows, inverse, (((1,), (1,)), ((), ())), precision=lax.Precision.HIGHEST)


def early_corner(child_piece, row_map, col_map, full_diagonal):
    n_row = lax.axis_size("row")
    n_col = lax.axis_size("col")
    n_sub = lax.axis_size("sub")
    rows_here, cols_here = child_piece.shape
    row_blocks = rows_here // BLOCK
    col_blocks = cols_here // BLOCK
    panel_blocks = PANEL // BLOCK
    first_rows = min(row_blocks, -(-panel_blocks // n_row))
    first_cols = min(col_blocks, -(-panel_blocks // n_col))
    piece = child_piece[: first_rows * BLOCK, : first_cols * BLOCK]
    pieces = lax.all_gather(piece, ("sub", "row", "col"))
    pieces = pieces.reshape(n_sub, n_row, n_col, first_rows, BLOCK, first_cols, BLOCK)
    pieces = pieces.transpose(0, 1, 3, 2, 5, 4, 6).reshape(
        n_sub, n_row * first_rows, n_col * first_cols, BLOCK, BLOCK
    )
    row_pos = (
        jnp.arange(n_row, dtype=jnp.int32)[:, None] * row_blocks
        + jnp.arange(first_rows, dtype=jnp.int32)[None, :]
    ).reshape(-1)
    col_pos = (
        jnp.arange(n_col, dtype=jnp.int32)[:, None] * col_blocks
        + jnp.arange(first_cols, dtype=jnp.int32)[None, :]
    ).reshape(-1)
    corner = jnp.zeros((panel_blocks + 1, panel_blocks + 1, BLOCK, BLOCK), jnp.float32)
    for which in range(n_sub):
        rb = row_map[which][row_pos]
        cb = col_map[which][col_pos]
        rb = jnp.where(rb < panel_blocks, rb, panel_blocks)
        cb = jnp.where(cb < panel_blocks, cb, panel_blocks)
        corner = corner.at[rb[:, None], cb[None, :]].add(pieces[which])
    corner = corner[:panel_blocks, :panel_blocks].transpose(0, 2, 1, 3).reshape(PANEL, PANEL)
    return corner + jnp.diag(full_diagonal[:PANEL])


def shards(child, row_map, col_map, own_diagonal, coupling):
    n_row = lax.axis_size("row")
    n_col = lax.axis_size("col")
    n_group = lax.axis_size(("sub", "col"))
    my_row = lax.axis_index("row")
    my_col = lax.axis_index("col")
    my_sub = lax.axis_index("sub")
    my_group = lax.axis_index(("sub", "col"))
    child_piece = child[0]
    rows_here, cols_here = child_piece.shape
    front_rows = FRONT // n_row
    front_cols = FRONT // n_group
    row_blocks = rows_here // BLOCK
    col_blocks = cols_here // BLOCK
    front_row_blocks = front_rows // BLOCK
    front_col_blocks = front_cols // BLOCK
    row_cap = min(row_blocks, (front_row_blocks + n_row - 1) // n_row)
    col_cap = min(col_blocks, (front_col_blocks + n_col - 1) // n_col)
    n_sub = lax.axis_size("sub")
    my_rows_map = lax.dynamic_index_in_dim(row_map, my_sub, 0, keepdims=False)
    my_cols_map = lax.dynamic_index_in_dim(col_map, my_sub, 0, keepdims=False)

    full_diagonal = from_root(own_diagonal[:PANEL], ("sub", "col"), 0)
    corner = early_corner(child_piece, row_map, col_map, full_diagonal)
    global_row = my_row * front_rows + jnp.arange(front_rows, dtype=jnp.int32)

    panel_blocks = PANEL // BLOCK
    first_cols = min(col_blocks, -(-panel_blocks // n_col))
    own_cands = child_piece[:, : first_cols * BLOCK].reshape(row_blocks, BLOCK, first_cols * BLOCK)
    pick_rows = sending_table(my_rows_map, my_row, row_blocks, front_row_blocks, n_row, row_cap)
    pick_rows = jnp.minimum(pick_rows, row_blocks - 1).reshape(n_row, row_cap)
    cand_send = own_cands.at[pick_rows].get(mode="promise_in_bounds")
    pieces = [lax.dynamic_index_in_dim(cand_send, my_row, 0, keepdims=False)]
    for shift in range(1, n_row):
        piece = lax.dynamic_index_in_dim(cand_send, (my_row + shift) % n_row, 0, keepdims=False)
        pieces.append(lax.ppermute(piece, "row", [(i, (i + shift) % n_row) for i in range(n_row)]))
    cand_got = jnp.stack(pieces).reshape(n_row * row_cap, BLOCK, first_cols * BLOCK)
    placement = receiving_table(
        my_rows_map, my_row, row_blocks, front_row_blocks, row_cap, 0, n_row * row_cap
    )
    row_valid = placement < n_row * row_cap
    source = jnp.minimum(placement, n_row * row_cap - 1) // row_cap
    placement = ((my_row - source) % n_row) * row_cap + placement % row_cap
    cand_rows = jnp.where(
        row_valid[:, None, None], cand_got.at[placement].get(mode="promise_in_bounds"), 0.0
    )
    cands = lax.all_gather(cand_rows, "col")
    cands = jnp.stack([cands, lax.ppermute(cands, "sub", [(0, 1), (1, 0)])])
    cands = cands.reshape(n_sub, n_col, front_row_blocks, BLOCK, first_cols, BLOCK)
    cands = cands.transpose(0, 1, 4, 2, 3, 5).reshape(
        n_sub, n_col * first_cols, front_row_blocks, BLOCK, BLOCK
    )
    cand_pos = (
        jnp.arange(n_col, dtype=jnp.int32)[:, None] * col_blocks
        + jnp.arange(first_cols, dtype=jnp.int32)[None, :]
    ).reshape(-1)
    panel_rows = None
    for which in range(n_sub):
        found = col_map[which][cand_pos][None, :] == jnp.arange(panel_blocks, dtype=jnp.int32)[:, None]
        pick = jnp.argmax(found, axis=1)
        mine = lax.dynamic_index_in_dim(cands, (which + my_sub) % n_sub, 0, keepdims=False)
        got = jnp.where(jnp.any(found, axis=1)[:, None, None, None], mine[pick], 0.0)
        panel_rows = got if panel_rows is None else panel_rows + got
    panel_rows = panel_rows.transpose(1, 2, 0, 3).reshape(front_rows, PANEL)
    panel_rows = panel_rows + jnp.where(global_row[:, None] >= PANEL, coupling, 0.0)
    panel_rows = panel_rows + jnp.where(
        global_row[:, None] == jnp.arange(PANEL, dtype=jnp.int32)[None, :], full_diagonal[None, :PANEL], 0.0
    )

    by_col = child_piece.reshape(rows_here, col_blocks, BLOCK)
    chosen = sending_table(my_cols_map, my_col, col_blocks, front_col_blocks, n_group, col_cap)
    chosen = jnp.minimum(chosen, col_blocks - 1).reshape(n_sub, n_col * col_cap)
    chosen = jnp.stack([chosen[1 - my_sub], chosen[my_sub]]).reshape(-1)
    outgoing = by_col.at[:, chosen].get(mode="promise_in_bounds")
    outgoing = outgoing.transpose(1, 0, 2).reshape(2, n_col, col_cap, rows_here, BLOCK)
    outgoing, corner = lax.optimization_barrier((outgoing, corner))
    lower, inverse = factor_corner(corner)
    other_half = lax.all_to_all(outgoing[0], "col", split_axis=0, concat_axis=0, tiled=True)
    other_half, lower, inverse, panel_rows = lax.optimization_barrier(
        (other_half, lower, inverse, panel_rows)
    )
    other_half = lax.ppermute(other_half, "sub", [(0, 1), (1, 0)])

    def row_sending(half, which):
        cols_of = lax.dynamic_index_in_dim(col_map, which, 0, keepdims=False)
        rows_of = lax.dynamic_index_in_dim(row_map, which, 0, keepdims=False)
        col_index = receiving_table(
            cols_of, my_group, col_blocks, front_col_blocks, col_cap, 0, n_col * col_cap
        )
        col_valid = col_index < n_col * col_cap
        col_index = jnp.minimum(col_index, n_col * col_cap - 1)
        row_index = sending_table(rows_of, my_row, row_blocks, front_row_blocks, n_row, row_cap)
        row_index = jnp.minimum(row_index, row_blocks - 1).reshape(n_row, row_cap)
        half = half.reshape(n_col * col_cap, row_blocks, BLOCK, BLOCK)
        sending = half.at[col_index[None, None, :], row_index[:, :, None]].get(
            mode="promise_in_bounds"
        )
        return sending, col_valid, rows_of

    def row_receiving(sending, col_valid, rows_of, by_permutes):
        placement = receiving_table(
            rows_of, my_row, row_blocks, front_row_blocks, row_cap, 0, n_row * row_cap
        )
        row_valid = placement < n_row * row_cap
        placement = jnp.minimum(placement, n_row * row_cap - 1)
        if by_permutes:
            pieces = [lax.dynamic_index_in_dim(sending, my_row, 0, keepdims=False)]
            for shift in range(1, n_row):
                piece = lax.dynamic_index_in_dim(sending, (my_row + shift) % n_row, 0, keepdims=False)
                pairs = [(i, (i + shift) % n_row) for i in range(n_row)]
                pieces.append(lax.ppermute(piece, "row", pairs))
            received = jnp.stack(pieces)
            source = placement // row_cap
            placement = ((my_row - source) % n_row) * row_cap + placement % row_cap
        else:
            received = lax.all_to_all(sending, "row", split_axis=0, concat_axis=0, tiled=True)
        received = received.reshape(n_row * row_cap, front_col_blocks, BLOCK, BLOCK)
        part = received.at[placement].get(mode="promise_in_bounds")
        keep = row_valid[:, None] & col_valid[None, :]
        return part, keep

    sending_other, col_valid_other, rows_other = row_sending(other_half, 1 - my_sub)
    sending_other, own_outgoing = lax.optimization_barrier((sending_other, outgoing[1]))
    part_other, keep_other = row_receiving(sending_other, col_valid_other, rows_other, True)
    own_half = lax.all_to_all(own_outgoing, "col", split_axis=0, concat_axis=0, tiled=True)
    own_half, part_other = lax.optimization_barrier((own_half, part_other))
    sending_own, col_valid_own, rows_own = row_sending(own_half, my_sub)
    part_own, keep_own = row_receiving(sending_own, col_valid_own, rows_own, False)
    assembled = jnp.where(keep_other[:, :, None, None], part_other, 0.0) + jnp.where(
        keep_own[:, :, None, None], part_own, 0.0
    )
    assembled = assembled.transpose(0, 2, 1, 3).reshape(front_rows, front_cols)

    global_col = my_group * front_cols + jnp.arange(front_cols, dtype=jnp.int32)
    on_diagonal = global_row[:, None] == global_col[None, :]
    assembled = assembled + jnp.where(on_diagonal, own_diagonal[None, :], 0.0)
    coupling_wide = jnp.concatenate(
        [coupling, jnp.zeros((front_rows, front_cols - PANEL), jnp.float32)], axis=1
    )
    coupling_mask = (global_row[:, None] >= PANEL) & (global_col[None, :] < PANEL)
    front_part = assembled + jnp.where(coupling_mask, coupling_wide, 0.0)
    theirs_start = my_group * front_cols % front_rows
    theirs_root = my_group * front_cols // front_rows
    own_rows = apply_inverse(panel_rows, inverse)
    top_rows = jnp.where(my_row == 0, lower, own_rows[:PANEL])
    own_rows = jnp.concatenate([top_rows, own_rows[PANEL:]], axis=0)
    theirs = lax.dynamic_slice_in_dim(own_rows, theirs_start, front_cols, 0)
    theirs = from_root(theirs, "row", theirs_root)
    update = lax.dot_general(
        own_rows, theirs, (((1,), (1,)), ((), ())), precision=lax.Precision.HIGHEST
    )
    panel_wide = jnp.concatenate(
        [own_rows, jnp.zeros((front_rows, front_cols - PANEL), jnp.float32)], axis=1
    )
    trailing = front_part - update
    result = jnp.where(
        global_col[None, :] < PANEL,
        panel_wide,
        jnp.where(global_row[:, None] < PANEL, 0.0, trailing),
    )
    return result


def solution(mesh):
    placed = (P("sub", "row", "col"), P(), P(), P(("sub", "col")), P("row", None))
    return jax.shard_map(
        shards, mesh=mesh, in_specs=placed, out_specs=P("row", ("sub", "col")), check_vma=False
    )
```

```python
import jax
import jax.numpy as jnp
from jax import lax
from jax.sharding import PartitionSpec as P

FRONT = 10240
PANEL = 512
BLOCK = 128


def from_root(value, axis, source):
    kept = jnp.where(lax.axis_index(axis) == source, value, 0).astype(value.dtype)
    return lax.psum(kept, axis)


def block_routes(parent_blocks, per_source, per_target):
    number = parent_blocks.shape[0]
    positions = jnp.arange(number, dtype=jnp.int32)
    source = positions // per_source
    target = parent_blocks // per_target
    earlier = (
        (source[:, None] == source[None, :])
        & (target[:, None] == target[None, :])
        & (positions[None, :] < positions[:, None])
    )
    slot_index = jnp.sum(earlier.astype(jnp.int32), axis=1)
    return (positions, source, target, slot_index, parent_blocks % per_target)


def sending_table(parent_blocks, own_index, per_source, per_target, targets, capacity):
    positions, source, target, slot_index, local_block = block_routes(
        parent_blocks, per_source, per_target
    )
    wanted = jnp.arange(targets * capacity, dtype=jnp.int32)
    matches = (source == own_index)[None, :] & (
        (target * capacity + slot_index)[None, :] == wanted[:, None]
    )
    within = positions % per_source
    return jnp.where(
        jnp.any(matches, axis=1),
        jnp.sum(jnp.where(matches, within[None, :], 0), axis=1),
        per_source,
    )


def receiving_table(parent_blocks, own_index, per_source, per_target, capacity, offset, empty_slot):
    positions, source, target, slot_index, local_block = block_routes(
        parent_blocks, per_source, per_target
    )
    wanted = jnp.arange(per_target, dtype=jnp.int32)
    matches = (target == own_index)[None, :] & (local_block[None, :] == wanted[:, None])
    flat_slot = (source + offset) * capacity + slot_index
    return jnp.where(
        jnp.any(matches, axis=1),
        jnp.sum(jnp.where(matches, flat_slot[None, :], 0), axis=1),
        empty_slot,
    )


def with_zero(blocks, axis):
    shape = list(blocks.shape)
    shape[axis] = 1
    return jnp.concatenate([blocks, jnp.zeros(shape, blocks.dtype)], axis=axis)


def symmetric_of(corner):
    return jnp.tril(corner) + jnp.tril(corner, -1).T


def factor_corner(corner):
    lower = jnp.linalg.cholesky(symmetric_of(corner))
    inverse = jax.scipy.linalg.solve_triangular(
        lower, jnp.eye(PANEL, dtype=jnp.float32), lower=True
    )
    return (lower, inverse)


def apply_inverse(rows, inverse):
    return lax.dot_general(rows, inverse, (((1,), (1,)), ((), ())), precision=lax.Precision.HIGHEST)


def early_corner(child_piece, row_map, col_map, full_diagonal):
    n_row = lax.axis_size("row")
    n_col = lax.axis_size("col")
    n_sub = lax.axis_size("sub")
    rows_here, cols_here = child_piece.shape
    row_blocks = rows_here // BLOCK
    col_blocks = cols_here // BLOCK
    panel_blocks = PANEL // BLOCK
    first_rows = min(row_blocks, -(-panel_blocks // n_row))
    first_cols = min(col_blocks, -(-panel_blocks // n_col))
    piece = child_piece[: first_rows * BLOCK, : first_cols * BLOCK]
    pieces = lax.all_gather(piece, ("sub", "row", "col"))
    pieces = pieces.reshape(n_sub, n_row, n_col, first_rows, BLOCK, first_cols, BLOCK)
    pieces = pieces.transpose(0, 1, 3, 2, 5, 4, 6).reshape(
        n_sub, n_row * first_rows, n_col * first_cols, BLOCK, BLOCK
    )
    row_pos = (
        jnp.arange(n_row, dtype=jnp.int32)[:, None] * row_blocks
        + jnp.arange(first_rows, dtype=jnp.int32)[None, :]
    ).reshape(-1)
    col_pos = (
        jnp.arange(n_col, dtype=jnp.int32)[:, None] * col_blocks
        + jnp.arange(first_cols, dtype=jnp.int32)[None, :]
    ).reshape(-1)
    corner = jnp.zeros((panel_blocks + 1, panel_blocks + 1, BLOCK, BLOCK), jnp.float32)
    for which in range(n_sub):
        rb = row_map[which][row_pos]
        cb = col_map[which][col_pos]
        rb = jnp.where(rb < panel_blocks, rb, panel_blocks)
        cb = jnp.where(cb < panel_blocks, cb, panel_blocks)
        corner = corner.at[rb[:, None], cb[None, :]].add(pieces[which])
    corner = corner[:panel_blocks, :panel_blocks].transpose(0, 2, 1, 3).reshape(PANEL, PANEL)
    return corner + jnp.diag(full_diagonal[:PANEL])


def shards(child, row_map, col_map, own_diagonal, coupling):
    n_row = lax.axis_size("row")
    n_col = lax.axis_size("col")
    n_group = lax.axis_size(("sub", "col"))
    my_row = lax.axis_index("row")
    my_col = lax.axis_index("col")
    my_sub = lax.axis_index("sub")
    my_group = lax.axis_index(("sub", "col"))
    child_piece = child[0]
    rows_here, cols_here = child_piece.shape
    front_rows = FRONT // n_row
    front_cols = FRONT // n_group
    row_blocks = rows_here // BLOCK
    col_blocks = cols_here // BLOCK
    front_row_blocks = front_rows // BLOCK
    front_col_blocks = front_cols // BLOCK
    row_cap = min(row_blocks, (front_row_blocks + n_row - 1) // n_row)
    col_cap = min(col_blocks, (front_col_blocks + n_col - 1) // n_col)
    n_sub = lax.axis_size("sub")
    my_rows_map = lax.dynamic_index_in_dim(row_map, my_sub, 0, keepdims=False)
    my_cols_map = lax.dynamic_index_in_dim(col_map, my_sub, 0, keepdims=False)

    full_diagonal = from_root(own_diagonal[:PANEL], ("sub", "col"), 0)
    corner = early_corner(child_piece, row_map, col_map, full_diagonal)
    global_row = my_row * front_rows + jnp.arange(front_rows, dtype=jnp.int32)

    panel_blocks = PANEL // BLOCK
    first_cols = min(col_blocks, -(-panel_blocks // n_col))
    own_cands = child_piece[:, : first_cols * BLOCK].reshape(row_blocks, BLOCK, first_cols * BLOCK)
    pick_rows = sending_table(my_rows_map, my_row, row_blocks, front_row_blocks, n_row, row_cap)
    pick_rows = jnp.minimum(pick_rows, row_blocks - 1).reshape(n_row, row_cap)
    cand_send = own_cands.at[pick_rows].get(mode="promise_in_bounds")
    pieces = [lax.dynamic_index_in_dim(cand_send, my_row, 0, keepdims=False)]
    for shift in range(1, n_row):
        piece = lax.dynamic_index_in_dim(cand_send, (my_row + shift) % n_row, 0, keepdims=False)
        pieces.append(lax.ppermute(piece, "row", [(i, (i + shift) % n_row) for i in range(n_row)]))
    cand_got = jnp.stack(pieces).reshape(n_row * row_cap, BLOCK, first_cols * BLOCK)
    placement = receiving_table(
        my_rows_map, my_row, row_blocks, front_row_blocks, row_cap, 0, n_row * row_cap
    )
    row_valid = placement < n_row * row_cap
    source = jnp.minimum(placement, n_row * row_cap - 1) // row_cap
    placement = ((my_row - source) % n_row) * row_cap + placement % row_cap
    cand_rows = jnp.where(
        row_valid[:, None, None], cand_got.at[placement].get(mode="promise_in_bounds"), 0.0
    )
    cands = lax.all_gather(cand_rows, "col")
    cands = jnp.stack([cands, lax.ppermute(cands, "sub", [(0, 1), (1, 0)])])
    cands = cands.reshape(n_sub, n_col, front_row_blocks, BLOCK, first_cols, BLOCK)
    cands = cands.transpose(0, 1, 4, 2, 3, 5).reshape(
        n_sub, n_col * first_cols, front_row_blocks, BLOCK, BLOCK
    )
    cand_pos = (
        jnp.arange(n_col, dtype=jnp.int32)[:, None] * col_blocks
        + jnp.arange(first_cols, dtype=jnp.int32)[None, :]
    ).reshape(-1)
    panel_rows = None
    for which in range(n_sub):
        found = col_map[which][cand_pos][None, :] == jnp.arange(panel_blocks, dtype=jnp.int32)[:, None]
        pick = jnp.argmax(found, axis=1)
        mine = lax.dynamic_index_in_dim(cands, (which + my_sub) % n_sub, 0, keepdims=False)
        got = jnp.where(jnp.any(found, axis=1)[:, None, None, None], mine[pick], 0.0)
        panel_rows = got if panel_rows is None else panel_rows + got
    panel_rows = panel_rows.transpose(1, 2, 0, 3).reshape(front_rows, PANEL)
    panel_rows = panel_rows + jnp.where(global_row[:, None] >= PANEL, coupling, 0.0)
    panel_rows = panel_rows + jnp.where(
        global_row[:, None] == jnp.arange(PANEL, dtype=jnp.int32)[None, :], full_diagonal[None, :PANEL], 0.0
    )

    by_col = child_piece.reshape(rows_here, col_blocks, BLOCK)
    chosen = sending_table(my_cols_map, my_col, col_blocks, front_col_blocks, n_group, col_cap)
    chosen = jnp.minimum(chosen, col_blocks - 1).reshape(n_sub, n_col * col_cap)
    chosen = jnp.stack([chosen[1 - my_sub], chosen[my_sub]]).reshape(-1)
    outgoing = by_col.at[:, chosen].get(mode="promise_in_bounds")
    outgoing = outgoing.transpose(1, 0, 2).reshape(2, n_col, col_cap, rows_here, BLOCK)
    outgoing, corner = lax.optimization_barrier((outgoing, corner))
    lower, inverse = factor_corner(corner)
    other_half = lax.all_to_all(outgoing[0], "col", split_axis=0, concat_axis=0, tiled=True)
    other_half, lower, inverse, panel_rows = lax.optimization_barrier(
        (other_half, lower, inverse, panel_rows)
    )
    other_half = lax.ppermute(other_half, "sub", [(0, 1), (1, 0)])

    def row_sending(half, which):
        cols_of = lax.dynamic_index_in_dim(col_map, which, 0, keepdims=False)
        rows_of = lax.dynamic_index_in_dim(row_map, which, 0, keepdims=False)
        col_index = receiving_table(
            cols_of, my_group, col_blocks, front_col_blocks, col_cap, 0, n_col * col_cap
        )
        col_valid = col_index < n_col * col_cap
        col_index = jnp.minimum(col_index, n_col * col_cap - 1)
        row_index = sending_table(rows_of, my_row, row_blocks, front_row_blocks, n_row, row_cap)
        row_index = jnp.minimum(row_index, row_blocks - 1).reshape(n_row, row_cap)
        half = half.reshape(n_col * col_cap, row_blocks, BLOCK, BLOCK)
        sending = half.at[col_index[None, None, :], row_index[:, :, None]].get(
            mode="promise_in_bounds"
        )
        return sending, col_valid, rows_of

    def row_receiving(sending, col_valid, rows_of, by_permutes):
        placement = receiving_table(
            rows_of, my_row, row_blocks, front_row_blocks, row_cap, 0, n_row * row_cap
        )
        row_valid = placement < n_row * row_cap
        placement = jnp.minimum(placement, n_row * row_cap - 1)
        if by_permutes:
            pieces = [lax.dynamic_index_in_dim(sending, my_row, 0, keepdims=False)]
            for shift in range(1, n_row):
                piece = lax.dynamic_index_in_dim(sending, (my_row + shift) % n_row, 0, keepdims=False)
                pairs = [(i, (i + shift) % n_row) for i in range(n_row)]
                pieces.append(lax.ppermute(piece, "row", pairs))
            received = jnp.stack(pieces)
            source = placement // row_cap
            placement = ((my_row - source) % n_row) * row_cap + placement % row_cap
        else:
            received = lax.all_to_all(sending, "row", split_axis=0, concat_axis=0, tiled=True)
        received = received.reshape(n_row * row_cap, front_col_blocks, BLOCK, BLOCK)
        part = received.at[placement].get(mode="promise_in_bounds")
        keep = row_valid[:, None] & col_valid[None, :]
        return part, keep

    sending_other, col_valid_other, rows_other = row_sending(other_half, 1 - my_sub)
    sending_other, own_outgoing = lax.optimization_barrier((sending_other, outgoing[1]))
    part_other, keep_other = row_receiving(sending_other, col_valid_other, rows_other, True)
    own_half = lax.all_to_all(own_outgoing, "col", split_axis=0, concat_axis=0, tiled=True)
    own_half, part_other = lax.optimization_barrier((own_half, part_other))
    theirs_start = my_group * front_cols % front_rows
    theirs_root = my_group * front_cols // front_rows
    own_rows = apply_inverse(panel_rows, inverse)
    top_rows = jnp.where(my_row == 0, lower, own_rows[:PANEL])
    own_rows = jnp.concatenate([top_rows, own_rows[PANEL:]], axis=0)
    theirs = lax.dynamic_slice_in_dim(own_rows, theirs_start, front_cols, 0)
    theirs = from_root(theirs, "row", theirs_root)
    update = lax.dot_general(
        own_rows, theirs, (((1,), (1,)), ((), ())), precision=lax.Precision.HIGHEST
    )
    sending_own, col_valid_own, rows_own = row_sending(own_half, my_sub)
    sending_own, update = lax.optimization_barrier((sending_own, update))
    part_own, keep_own = row_receiving(sending_own, col_valid_own, rows_own, False)
    assembled = jnp.where(keep_other[:, :, None, None], part_other, 0.0) + jnp.where(
        keep_own[:, :, None, None], part_own, 0.0
    )
    assembled = assembled.transpose(0, 2, 1, 3).reshape(front_rows, front_cols)

    global_col = my_group * front_cols + jnp.arange(front_cols, dtype=jnp.int32)
    on_diagonal = global_row[:, None] == global_col[None, :]
    assembled = assembled + jnp.where(on_diagonal, own_diagonal[None, :], 0.0)
    coupling_wide = jnp.concatenate(
        [coupling, jnp.zeros((front_rows, front_cols - PANEL), jnp.float32)], axis=1
    )
    coupling_mask = (global_row[:, None] >= PANEL) & (global_col[None, :] < PANEL)
    front_part = assembled + jnp.where(coupling_mask, coupling_wide, 0.0)
    panel_wide = jnp.concatenate(
        [own_rows, jnp.zeros((front_rows, front_cols - PANEL), jnp.float32)], axis=1
    )
    trailing = front_part - update
    result = jnp.where(
        global_col[None, :] < PANEL,
        panel_wide,
        jnp.where(global_row[:, None] < PANEL, 0.0, trailing),
    )
    return result


def solution(mesh):
    placed = (P("sub", "row", "col"), P(), P(), P(("sub", "col")), P("row", None))
    return jax.shard_map(
        shards, mesh=mesh, in_specs=placed, out_specs=P("row", ("sub", "col")), check_vma=False
    )
```

```python
import jax
import jax.numpy as jnp
from jax import lax
from jax.sharding import PartitionSpec as P

FRONT = 10240
PANEL = 512
BLOCK = 128


def from_root(value, axis, source):
    kept = jnp.where(lax.axis_index(axis) == source, value, 0).astype(value.dtype)
    return lax.psum(kept, axis)


def block_routes(parent_blocks, per_source, per_target):
    number = parent_blocks.shape[0]
    positions = jnp.arange(number, dtype=jnp.int32)
    source = positions // per_source
    target = parent_blocks // per_target
    earlier = (
        (source[:, None] == source[None, :])
        & (target[:, None] == target[None, :])
        & (positions[None, :] < positions[:, None])
    )
    slot_index = jnp.sum(earlier.astype(jnp.int32), axis=1)
    return (positions, source, target, slot_index, parent_blocks % per_target)


def sending_table(parent_blocks, own_index, per_source, per_target, targets, capacity):
    positions, source, target, slot_index, local_block = block_routes(
        parent_blocks, per_source, per_target
    )
    wanted = jnp.arange(targets * capacity, dtype=jnp.int32)
    matches = (source == own_index)[None, :] & (
        (target * capacity + slot_index)[None, :] == wanted[:, None]
    )
    within = positions % per_source
    return jnp.where(
        jnp.any(matches, axis=1),
        jnp.sum(jnp.where(matches, within[None, :], 0), axis=1),
        per_source,
    )


def receiving_table(parent_blocks, own_index, per_source, per_target, capacity, offset, empty_slot):
    positions, source, target, slot_index, local_block = block_routes(
        parent_blocks, per_source, per_target
    )
    wanted = jnp.arange(per_target, dtype=jnp.int32)
    matches = (target == own_index)[None, :] & (local_block[None, :] == wanted[:, None])
    flat_slot = (source + offset) * capacity + slot_index
    return jnp.where(
        jnp.any(matches, axis=1),
        jnp.sum(jnp.where(matches, flat_slot[None, :], 0), axis=1),
        empty_slot,
    )


def with_zero(blocks, axis):
    shape = list(blocks.shape)
    shape[axis] = 1
    return jnp.concatenate([blocks, jnp.zeros(shape, blocks.dtype)], axis=axis)


def symmetric_of(corner):
    return jnp.tril(corner) + jnp.tril(corner, -1).T


def factor_corner(corner):
    lower = jnp.linalg.cholesky(symmetric_of(corner))
    inverse = jax.scipy.linalg.solve_triangular(
        lower, jnp.eye(PANEL, dtype=jnp.float32), lower=True
    )
    return (lower, inverse)


def apply_inverse(rows, inverse):
    return lax.dot_general(rows, inverse, (((1,), (1,)), ((), ())), precision=lax.Precision.HIGHEST)


def early_corner(child_piece, row_map, col_map, full_diagonal):
    n_row = lax.axis_size("row")
    n_col = lax.axis_size("col")
    n_sub = lax.axis_size("sub")
    rows_here, cols_here = child_piece.shape
    row_blocks = rows_here // BLOCK
    col_blocks = cols_here // BLOCK
    panel_blocks = PANEL // BLOCK
    first_rows = min(row_blocks, -(-panel_blocks // n_row))
    first_cols = min(col_blocks, -(-panel_blocks // n_col))
    piece = child_piece[: first_rows * BLOCK, : first_cols * BLOCK]
    pieces = lax.all_gather(piece, ("sub", "row", "col"))
    pieces = pieces.reshape(n_sub, n_row, n_col, first_rows, BLOCK, first_cols, BLOCK)
    pieces = pieces.transpose(0, 1, 3, 2, 5, 4, 6).reshape(
        n_sub, n_row * first_rows, n_col * first_cols, BLOCK, BLOCK
    )
    row_pos = (
        jnp.arange(n_row, dtype=jnp.int32)[:, None] * row_blocks
        + jnp.arange(first_rows, dtype=jnp.int32)[None, :]
    ).reshape(-1)
    col_pos = (
        jnp.arange(n_col, dtype=jnp.int32)[:, None] * col_blocks
        + jnp.arange(first_cols, dtype=jnp.int32)[None, :]
    ).reshape(-1)
    corner = jnp.zeros((panel_blocks + 1, panel_blocks + 1, BLOCK, BLOCK), jnp.float32)
    for which in range(n_sub):
        rb = row_map[which][row_pos]
        cb = col_map[which][col_pos]
        rb = jnp.where(rb < panel_blocks, rb, panel_blocks)
        cb = jnp.where(cb < panel_blocks, cb, panel_blocks)
        corner = corner.at[rb[:, None], cb[None, :]].add(pieces[which])
    corner = corner[:panel_blocks, :panel_blocks].transpose(0, 2, 1, 3).reshape(PANEL, PANEL)
    return corner + jnp.diag(full_diagonal[:PANEL])


def shards(child, row_map, col_map, own_diagonal, coupling):
    n_row = lax.axis_size("row")
    n_col = lax.axis_size("col")
    n_group = lax.axis_size(("sub", "col"))
    my_row = lax.axis_index("row")
    my_col = lax.axis_index("col")
    my_sub = lax.axis_index("sub")
    my_group = lax.axis_index(("sub", "col"))
    child_piece = child[0]
    rows_here, cols_here = child_piece.shape
    front_rows = FRONT // n_row
    front_cols = FRONT // n_group
    row_blocks = rows_here // BLOCK
    col_blocks = cols_here // BLOCK
    front_row_blocks = front_rows // BLOCK
    front_col_blocks = front_cols // BLOCK
    row_cap = min(row_blocks, (front_row_blocks + n_row - 1) // n_row)
    col_cap = min(col_blocks, (front_col_blocks + n_col - 1) // n_col)
    n_sub = lax.axis_size("sub")
    my_rows_map = lax.dynamic_index_in_dim(row_map, my_sub, 0, keepdims=False)
    my_cols_map = lax.dynamic_index_in_dim(col_map, my_sub, 0, keepdims=False)

    full_diagonal = from_root(own_diagonal[:PANEL], ("sub", "col"), 0)
    corner = early_corner(child_piece, row_map, col_map, full_diagonal)
    global_row = my_row * front_rows + jnp.arange(front_rows, dtype=jnp.int32)

    panel_blocks = PANEL // BLOCK
    first_cols = min(col_blocks, -(-panel_blocks // n_col))
    own_cands = child_piece[:, : first_cols * BLOCK].reshape(row_blocks, BLOCK, first_cols * BLOCK)
    pick_rows = sending_table(my_rows_map, my_row, row_blocks, front_row_blocks, n_row, row_cap)
    pick_rows = jnp.minimum(pick_rows, row_blocks - 1).reshape(n_row, row_cap)
    cand_send = own_cands.at[pick_rows].get(mode="promise_in_bounds")
    pieces = [lax.dynamic_index_in_dim(cand_send, my_row, 0, keepdims=False)]
    for shift in range(1, n_row):
        piece = lax.dynamic_index_in_dim(cand_send, (my_row + shift) % n_row, 0, keepdims=False)
        pieces.append(lax.ppermute(piece, "row", [(i, (i + shift) % n_row) for i in range(n_row)]))
    cand_got = jnp.stack(pieces).reshape(n_row * row_cap, BLOCK, first_cols * BLOCK)
    placement = receiving_table(
        my_rows_map, my_row, row_blocks, front_row_blocks, row_cap, 0, n_row * row_cap
    )
    row_valid = placement < n_row * row_cap
    source = jnp.minimum(placement, n_row * row_cap - 1) // row_cap
    placement = ((my_row - source) % n_row) * row_cap + placement % row_cap
    cand_rows = jnp.where(
        row_valid[:, None, None], cand_got.at[placement].get(mode="promise_in_bounds"), 0.0
    )
    cands = lax.all_gather(cand_rows, "col")
    cands = jnp.stack([cands, lax.ppermute(cands, "sub", [(0, 1), (1, 0)])])
    cands = cands.reshape(n_sub, n_col, front_row_blocks, BLOCK, first_cols, BLOCK)
    cands = cands.transpose(0, 1, 4, 2, 3, 5).reshape(
        n_sub, n_col * first_cols, front_row_blocks, BLOCK, BLOCK
    )
    cand_pos = (
        jnp.arange(n_col, dtype=jnp.int32)[:, None] * col_blocks
        + jnp.arange(first_cols, dtype=jnp.int32)[None, :]
    ).reshape(-1)
    panel_rows = None
    for which in range(n_sub):
        found = col_map[which][cand_pos][None, :] == jnp.arange(panel_blocks, dtype=jnp.int32)[:, None]
        pick = jnp.argmax(found, axis=1)
        mine = lax.dynamic_index_in_dim(cands, (which + my_sub) % n_sub, 0, keepdims=False)
        got = jnp.where(jnp.any(found, axis=1)[:, None, None, None], mine[pick], 0.0)
        panel_rows = got if panel_rows is None else panel_rows + got
    panel_rows = panel_rows.transpose(1, 2, 0, 3).reshape(front_rows, PANEL)
    panel_rows = panel_rows + jnp.where(global_row[:, None] >= PANEL, coupling, 0.0)
    panel_rows = panel_rows + jnp.where(
        global_row[:, None] == jnp.arange(PANEL, dtype=jnp.int32)[None, :], full_diagonal[None, :PANEL], 0.0
    )

    by_col = child_piece.reshape(rows_here, col_blocks, BLOCK)
    chosen = sending_table(my_cols_map, my_col, col_blocks, front_col_blocks, n_group, col_cap)
    chosen = jnp.minimum(chosen, col_blocks - 1).reshape(n_sub, n_col * col_cap)
    chosen = jnp.stack([chosen[1 - my_sub], chosen[my_sub]]).reshape(-1)
    outgoing = by_col.at[:, chosen].get(mode="promise_in_bounds")
    outgoing = outgoing.transpose(1, 0, 2).reshape(2, n_col, col_cap, rows_here, BLOCK)
    outgoing, corner = lax.optimization_barrier((outgoing, corner))
    lower, inverse = factor_corner(corner)
    other_half = lax.all_to_all(outgoing[0], "col", split_axis=0, concat_axis=0, tiled=True)
    other_half, lower, inverse, panel_rows = lax.optimization_barrier(
        (other_half, lower, inverse, panel_rows)
    )
    other_half = lax.ppermute(other_half, "sub", [(0, 1), (1, 0)])

    def row_sending(half, which):
        cols_of = lax.dynamic_index_in_dim(col_map, which, 0, keepdims=False)
        rows_of = lax.dynamic_index_in_dim(row_map, which, 0, keepdims=False)
        col_index = receiving_table(
            cols_of, my_group, col_blocks, front_col_blocks, col_cap, 0, n_col * col_cap
        )
        col_valid = col_index < n_col * col_cap
        col_index = jnp.minimum(col_index, n_col * col_cap - 1)
        row_index = sending_table(rows_of, my_row, row_blocks, front_row_blocks, n_row, row_cap)
        row_index = jnp.minimum(row_index, row_blocks - 1).reshape(n_row, row_cap)
        half = half.reshape(n_col * col_cap, row_blocks, BLOCK, BLOCK)
        sending = half.at[col_index[None, None, :], row_index[:, :, None]].get(
            mode="promise_in_bounds"
        )
        return sending, col_valid, rows_of

    def row_receiving(sending, col_valid, rows_of, by_permutes, extra=None):
        placement = receiving_table(
            rows_of, my_row, row_blocks, front_row_blocks, row_cap, 0, n_row * row_cap
        )
        row_valid = placement < n_row * row_cap
        placement = jnp.minimum(placement, n_row * row_cap - 1)
        if by_permutes:
            pieces = [lax.dynamic_index_in_dim(sending, my_row, 0, keepdims=False)]
            for shift in range(1, n_row):
                piece = lax.dynamic_index_in_dim(sending, (my_row + shift) % n_row, 0, keepdims=False)
                pairs = [(i, (i + shift) % n_row) for i in range(n_row)]
                pieces.append(lax.ppermute(piece, "row", pairs))
            received = jnp.stack(pieces)
            source = placement // row_cap
            placement = ((my_row - source) % n_row) * row_cap + placement % row_cap
        else:
            received = lax.all_to_all(sending, "row", split_axis=0, concat_axis=0, tiled=True)
            received, extra = lax.optimization_barrier((received, extra))
        received = received.reshape(n_row * row_cap, front_col_blocks, BLOCK, BLOCK)
        part = received.at[placement].get(mode="promise_in_bounds")
        keep = row_valid[:, None] & col_valid[None, :]
        return part, keep, extra

    sending_other, col_valid_other, rows_other = row_sending(other_half, 1 - my_sub)
    sending_other, own_outgoing = lax.optimization_barrier((sending_other, outgoing[1]))
    part_other, keep_other, _ = row_receiving(sending_other, col_valid_other, rows_other, True)
    own_half = lax.all_to_all(own_outgoing, "col", split_axis=0, concat_axis=0, tiled=True)
    own_half, part_other = lax.optimization_barrier((own_half, part_other))
    sending_own, col_valid_own, rows_own = row_sending(own_half, my_sub)
    theirs_start = my_group * front_cols % front_rows
    theirs_root = my_group * front_cols // front_rows
    own_rows = apply_inverse(panel_rows, inverse)
    top_rows = jnp.where(my_row == 0, lower, own_rows[:PANEL])
    own_rows = jnp.concatenate([top_rows, own_rows[PANEL:]], axis=0)
    theirs = lax.dynamic_slice_in_dim(own_rows, theirs_start, front_cols, 0)
    theirs = from_root(theirs, "row", theirs_root)
    update = lax.dot_general(
        own_rows, theirs, (((1,), (1,)), ((), ())), precision=lax.Precision.HIGHEST
    )
    part_own, keep_own, update = row_receiving(
        sending_own, col_valid_own, rows_own, False, update
    )
    assembled = jnp.where(keep_other[:, :, None, None], part_other, 0.0) + jnp.where(
        keep_own[:, :, None, None], part_own, 0.0
    )
    assembled = assembled.transpose(0, 2, 1, 3).reshape(front_rows, front_cols)

    global_col = my_group * front_cols + jnp.arange(front_cols, dtype=jnp.int32)
    on_diagonal = global_row[:, None] == global_col[None, :]
    assembled = assembled + jnp.where(on_diagonal, own_diagonal[None, :], 0.0)
    coupling_wide = jnp.concatenate(
        [coupling, jnp.zeros((front_rows, front_cols - PANEL), jnp.float32)], axis=1
    )
    coupling_mask = (global_row[:, None] >= PANEL) & (global_col[None, :] < PANEL)
    front_part = assembled + jnp.where(coupling_mask, coupling_wide, 0.0)
    panel_wide = jnp.concatenate(
        [own_rows, jnp.zeros((front_rows, front_cols - PANEL), jnp.float32)], axis=1
    )
    trailing = front_part - update
    result = jnp.where(
        global_col[None, :] < PANEL,
        panel_wide,
        jnp.where(global_row[:, None] < PANEL, 0.0, trailing),
    )
    return result


def solution(mesh):
    placed = (P("sub", "row", "col"), P(), P(), P(("sub", "col")), P("row", None))
    return jax.shard_map(
        shards, mesh=mesh, in_specs=placed, out_specs=P("row", ("sub", "col")), check_vma=False
    )
```

```python
import jax
import jax.numpy as jnp
from jax import lax
from jax.sharding import PartitionSpec as P

FRONT = 10240
PANEL = 512
BLOCK = 128


def from_root(value, axis, source):
    kept = jnp.where(lax.axis_index(axis) == source, value, 0).astype(value.dtype)
    return lax.psum(kept, axis)


def block_routes(parent_blocks, per_source, per_target):
    number = parent_blocks.shape[0]
    positions = jnp.arange(number, dtype=jnp.int32)
    source = positions // per_source
    target = parent_blocks // per_target
    earlier = (
        (source[:, None] == source[None, :])
        & (target[:, None] == target[None, :])
        & (positions[None, :] < positions[:, None])
    )
    slot_index = jnp.sum(earlier.astype(jnp.int32), axis=1)
    return (positions, source, target, slot_index, parent_blocks % per_target)


def sending_table(parent_blocks, own_index, per_source, per_target, targets, capacity):
    positions, source, target, slot_index, local_block = block_routes(
        parent_blocks, per_source, per_target
    )
    wanted = jnp.arange(targets * capacity, dtype=jnp.int32)
    matches = (source == own_index)[None, :] & (
        (target * capacity + slot_index)[None, :] == wanted[:, None]
    )
    within = positions % per_source
    return jnp.where(
        jnp.any(matches, axis=1),
        jnp.sum(jnp.where(matches, within[None, :], 0), axis=1),
        per_source,
    )


def receiving_table(parent_blocks, own_index, per_source, per_target, capacity, offset, empty_slot):
    positions, source, target, slot_index, local_block = block_routes(
        parent_blocks, per_source, per_target
    )
    wanted = jnp.arange(per_target, dtype=jnp.int32)
    matches = (target == own_index)[None, :] & (local_block[None, :] == wanted[:, None])
    flat_slot = (source + offset) * capacity + slot_index
    return jnp.where(
        jnp.any(matches, axis=1),
        jnp.sum(jnp.where(matches, flat_slot[None, :], 0), axis=1),
        empty_slot,
    )


def with_zero(blocks, axis):
    shape = list(blocks.shape)
    shape[axis] = 1
    return jnp.concatenate([blocks, jnp.zeros(shape, blocks.dtype)], axis=axis)


def symmetric_of(corner):
    return jnp.tril(corner) + jnp.tril(corner, -1).T


def factor_corner(corner):
    lower = jnp.linalg.cholesky(symmetric_of(corner))
    inverse = jax.scipy.linalg.solve_triangular(
        lower, jnp.eye(PANEL, dtype=jnp.float32), lower=True
    )
    return (lower, inverse)


def apply_inverse(rows, inverse):
    return lax.dot_general(rows, inverse, (((1,), (1,)), ((), ())), precision=lax.Precision.HIGHEST)


def early_corner(child_piece, row_map, col_map, full_diagonal):
    n_row = lax.axis_size("row")
    n_col = lax.axis_size("col")
    n_sub = lax.axis_size("sub")
    rows_here, cols_here = child_piece.shape
    row_blocks = rows_here // BLOCK
    col_blocks = cols_here // BLOCK
    panel_blocks = PANEL // BLOCK
    first_rows = min(row_blocks, -(-panel_blocks // n_row))
    first_cols = min(col_blocks, -(-panel_blocks // n_col))
    piece = child_piece[: first_rows * BLOCK, : first_cols * BLOCK]
    pieces = lax.all_gather(piece, ("sub", "row", "col"))
    pieces = pieces.reshape(n_sub, n_row, n_col, first_rows, BLOCK, first_cols, BLOCK)
    pieces = pieces.transpose(0, 1, 3, 2, 5, 4, 6).reshape(
        n_sub, n_row * first_rows, n_col * first_cols, BLOCK, BLOCK
    )
    row_pos = (
        jnp.arange(n_row, dtype=jnp.int32)[:, None] * row_blocks
        + jnp.arange(first_rows, dtype=jnp.int32)[None, :]
    ).reshape(-1)
    col_pos = (
        jnp.arange(n_col, dtype=jnp.int32)[:, None] * col_blocks
        + jnp.arange(first_cols, dtype=jnp.int32)[None, :]
    ).reshape(-1)
    corner = jnp.zeros((panel_blocks + 1, panel_blocks + 1, BLOCK, BLOCK), jnp.float32)
    for which in range(n_sub):
        rb = row_map[which][row_pos]
        cb = col_map[which][col_pos]
        rb = jnp.where(rb < panel_blocks, rb, panel_blocks)
        cb = jnp.where(cb < panel_blocks, cb, panel_blocks)
        corner = corner.at[rb[:, None], cb[None, :]].add(pieces[which])
    corner = corner[:panel_blocks, :panel_blocks].transpose(0, 2, 1, 3).reshape(PANEL, PANEL)
    return corner + jnp.diag(full_diagonal[:PANEL])


def shards(child, row_map, col_map, own_diagonal, coupling):
    n_row = lax.axis_size("row")
    n_col = lax.axis_size("col")
    n_group = lax.axis_size(("sub", "col"))
    my_row = lax.axis_index("row")
    my_col = lax.axis_index("col")
    my_sub = lax.axis_index("sub")
    my_group = lax.axis_index(("sub", "col"))
    child_piece = child[0]
    rows_here, cols_here = child_piece.shape
    front_rows = FRONT // n_row
    front_cols = FRONT // n_group
    row_blocks = rows_here // BLOCK
    col_blocks = cols_here // BLOCK
    front_row_blocks = front_rows // BLOCK
    front_col_blocks = front_cols // BLOCK
    row_cap = min(row_blocks, (front_row_blocks + n_row - 1) // n_row)
    col_cap = min(col_blocks, (front_col_blocks + n_col - 1) // n_col)
    n_sub = lax.axis_size("sub")
    my_rows_map = lax.dynamic_index_in_dim(row_map, my_sub, 0, keepdims=False)
    my_cols_map = lax.dynamic_index_in_dim(col_map, my_sub, 0, keepdims=False)

    full_diagonal = from_root(own_diagonal[:PANEL], ("sub", "col"), 0)
    corner = early_corner(child_piece, row_map, col_map, full_diagonal)
    global_row = my_row * front_rows + jnp.arange(front_rows, dtype=jnp.int32)

    panel_blocks = PANEL // BLOCK
    first_cols = min(col_blocks, -(-panel_blocks // n_col))
    own_cands = child_piece[:, : first_cols * BLOCK].reshape(row_blocks, BLOCK, first_cols * BLOCK)
    pick_rows = sending_table(my_rows_map, my_row, row_blocks, front_row_blocks, n_row, row_cap)
    pick_rows = jnp.minimum(pick_rows, row_blocks - 1).reshape(n_row, row_cap)
    cand_send = own_cands.at[pick_rows].get(mode="promise_in_bounds")
    pieces = [lax.dynamic_index_in_dim(cand_send, my_row, 0, keepdims=False)]
    for shift in range(1, n_row):
        piece = lax.dynamic_index_in_dim(cand_send, (my_row + shift) % n_row, 0, keepdims=False)
        pieces.append(lax.ppermute(piece, "row", [(i, (i + shift) % n_row) for i in range(n_row)]))
    cand_got = jnp.stack(pieces).reshape(n_row * row_cap, BLOCK, first_cols * BLOCK)
    placement = receiving_table(
        my_rows_map, my_row, row_blocks, front_row_blocks, row_cap, 0, n_row * row_cap
    )
    row_valid = placement < n_row * row_cap
    source = jnp.minimum(placement, n_row * row_cap - 1) // row_cap
    placement = ((my_row - source) % n_row) * row_cap + placement % row_cap
    cand_rows = jnp.where(
        row_valid[:, None, None], cand_got.at[placement].get(mode="promise_in_bounds"), 0.0
    )
    cands = lax.all_gather(cand_rows, "col")
    cands = jnp.stack([cands, lax.ppermute(cands, "sub", [(0, 1), (1, 0)])])
    cands = cands.reshape(n_sub, n_col, front_row_blocks, BLOCK, first_cols, BLOCK)
    cands = cands.transpose(0, 1, 4, 2, 3, 5).reshape(
        n_sub, n_col * first_cols, front_row_blocks, BLOCK, BLOCK
    )
    cand_pos = (
        jnp.arange(n_col, dtype=jnp.int32)[:, None] * col_blocks
        + jnp.arange(first_cols, dtype=jnp.int32)[None, :]
    ).reshape(-1)
    panel_rows = None
    for which in range(n_sub):
        found = col_map[which][cand_pos][None, :] == jnp.arange(panel_blocks, dtype=jnp.int32)[:, None]
        pick = jnp.argmax(found, axis=1)
        mine = lax.dynamic_index_in_dim(cands, (which + my_sub) % n_sub, 0, keepdims=False)
        got = jnp.where(jnp.any(found, axis=1)[:, None, None, None], mine[pick], 0.0)
        panel_rows = got if panel_rows is None else panel_rows + got
    panel_rows = panel_rows.transpose(1, 2, 0, 3).reshape(front_rows, PANEL)
    panel_rows = panel_rows + jnp.where(global_row[:, None] >= PANEL, coupling, 0.0)
    panel_rows = panel_rows + jnp.where(
        global_row[:, None] == jnp.arange(PANEL, dtype=jnp.int32)[None, :], full_diagonal[None, :PANEL], 0.0
    )

    by_col = child_piece.reshape(rows_here, col_blocks, BLOCK)
    chosen = sending_table(my_cols_map, my_col, col_blocks, front_col_blocks, n_group, col_cap)
    chosen = jnp.minimum(chosen, col_blocks - 1).reshape(n_sub, n_col * col_cap)
    chosen = jnp.stack([chosen[1 - my_sub], chosen[my_sub]]).reshape(-1)
    outgoing = by_col.at[:, chosen].get(mode="promise_in_bounds")
    outgoing = outgoing.transpose(1, 0, 2).reshape(2, n_col, col_cap, rows_here, BLOCK)
    outgoing, corner = lax.optimization_barrier((outgoing, corner))
    lower, inverse = factor_corner(corner)
    other_half = lax.all_to_all(outgoing[0], "col", split_axis=0, concat_axis=0, tiled=True)
    other_half, lower, inverse, panel_rows = lax.optimization_barrier(
        (other_half, lower, inverse, panel_rows)
    )
    other_half = lax.ppermute(other_half, "sub", [(0, 1), (1, 0)])

    def row_sending(half, which):
        cols_of = lax.dynamic_index_in_dim(col_map, which, 0, keepdims=False)
        rows_of = lax.dynamic_index_in_dim(row_map, which, 0, keepdims=False)
        col_index = receiving_table(
            cols_of, my_group, col_blocks, front_col_blocks, col_cap, 0, n_col * col_cap
        )
        col_valid = col_index < n_col * col_cap
        col_index = jnp.minimum(col_index, n_col * col_cap - 1)
        row_index = sending_table(rows_of, my_row, row_blocks, front_row_blocks, n_row, row_cap)
        row_index = jnp.minimum(row_index, row_blocks - 1).reshape(n_row, row_cap)
        half = half.reshape(n_col * col_cap, row_blocks, BLOCK, BLOCK)
        sending = half.at[col_index[None, None, :], row_index[:, :, None]].get(
            mode="promise_in_bounds"
        )
        return sending, col_valid, rows_of

    def row_receiving(sending, col_valid, rows_of, by_permutes):
        placement = receiving_table(
            rows_of, my_row, row_blocks, front_row_blocks, row_cap, 0, n_row * row_cap
        )
        row_valid = placement < n_row * row_cap
        placement = jnp.minimum(placement, n_row * row_cap - 1)
        if by_permutes:
            pieces = [lax.dynamic_index_in_dim(sending, my_row, 0, keepdims=False)]
            for shift in range(1, n_row):
                piece = lax.dynamic_index_in_dim(sending, (my_row + shift) % n_row, 0, keepdims=False)
                pairs = [(i, (i + shift) % n_row) for i in range(n_row)]
                pieces.append(lax.ppermute(piece, "row", pairs))
            received = jnp.stack(pieces)
            source = placement // row_cap
            placement = ((my_row - source) % n_row) * row_cap + placement % row_cap
        else:
            received = lax.all_to_all(sending, "row", split_axis=0, concat_axis=0, tiled=True)
        received = received.reshape(n_row * row_cap, front_col_blocks, BLOCK, BLOCK)
        part = received.at[placement].get(mode="promise_in_bounds")
        keep = row_valid[:, None] & col_valid[None, :]
        return part, keep

    sending_other, col_valid_other, rows_other = row_sending(other_half, 1 - my_sub)
    sending_other, own_outgoing = lax.optimization_barrier((sending_other, outgoing[1]))
    part_other, keep_other = row_receiving(sending_other, col_valid_other, rows_other, True)
    own_half = lax.all_to_all(own_outgoing, "col", split_axis=0, concat_axis=0, tiled=True)
    theirs_start = my_group * front_cols % front_rows
    theirs_root = my_group * front_cols // front_rows
    own_rows = apply_inverse(panel_rows, inverse)
    top_rows = jnp.where(my_row == 0, lower, own_rows[:PANEL])
    own_rows = jnp.concatenate([top_rows, own_rows[PANEL:]], axis=0)
    theirs = lax.dynamic_slice_in_dim(own_rows, theirs_start, front_cols, 0)
    theirs = from_root(theirs, "row", theirs_root)
    own_half, part_other, theirs = lax.optimization_barrier((own_half, part_other, theirs))
    sending_own, col_valid_own, rows_own = row_sending(own_half, my_sub)
    part_own, keep_own = row_receiving(sending_own, col_valid_own, rows_own, False)
    assembled = jnp.where(keep_other[:, :, None, None], part_other, 0.0) + jnp.where(
        keep_own[:, :, None, None], part_own, 0.0
    )
    assembled = assembled.transpose(0, 2, 1, 3).reshape(front_rows, front_cols)

    global_col = my_group * front_cols + jnp.arange(front_cols, dtype=jnp.int32)
    on_diagonal = global_row[:, None] == global_col[None, :]
    assembled = assembled + jnp.where(on_diagonal, own_diagonal[None, :], 0.0)
    coupling_wide = jnp.concatenate(
        [coupling, jnp.zeros((front_rows, front_cols - PANEL), jnp.float32)], axis=1
    )
    coupling_mask = (global_row[:, None] >= PANEL) & (global_col[None, :] < PANEL)
    front_part = assembled + jnp.where(coupling_mask, coupling_wide, 0.0)
    update = lax.dot_general(
        own_rows, theirs, (((1,), (1,)), ((), ())), precision=lax.Precision.HIGHEST
    )
    panel_wide = jnp.concatenate(
        [own_rows, jnp.zeros((front_rows, front_cols - PANEL), jnp.float32)], axis=1
    )
    trailing = front_part - update
    result = jnp.where(
        global_col[None, :] < PANEL,
        panel_wide,
        jnp.where(global_row[:, None] < PANEL, 0.0, trailing),
    )
    return result


def solution(mesh):
    placed = (P("sub", "row", "col"), P(), P(), P(("sub", "col")), P("row", None))
    return jax.shard_map(
        shards, mesh=mesh, in_specs=placed, out_specs=P("row", ("sub", "col")), check_vma=False
    )
```

```python
import jax
import jax.numpy as jnp
from jax import lax
from jax.sharding import PartitionSpec as P

FRONT = 10240
PANEL = 512
BLOCK = 128


def from_root(value, axis, source):
    kept = jnp.where(lax.axis_index(axis) == source, value, 0).astype(value.dtype)
    return lax.psum(kept, axis)


def block_routes(parent_blocks, per_source, per_target):
    number = parent_blocks.shape[0]
    positions = jnp.arange(number, dtype=jnp.int32)
    source = positions // per_source
    target = parent_blocks // per_target
    earlier = (
        (source[:, None] == source[None, :])
        & (target[:, None] == target[None, :])
        & (positions[None, :] < positions[:, None])
    )
    slot_index = jnp.sum(earlier.astype(jnp.int32), axis=1)
    return (positions, source, target, slot_index, parent_blocks % per_target)


def sending_table(parent_blocks, own_index, per_source, per_target, targets, capacity):
    positions, source, target, slot_index, local_block = block_routes(
        parent_blocks, per_source, per_target
    )
    wanted = jnp.arange(targets * capacity, dtype=jnp.int32)
    matches = (source == own_index)[None, :] & (
        (target * capacity + slot_index)[None, :] == wanted[:, None]
    )
    within = positions % per_source
    return jnp.where(
        jnp.any(matches, axis=1),
        jnp.sum(jnp.where(matches, within[None, :], 0), axis=1),
        per_source,
    )


def receiving_table(parent_blocks, own_index, per_source, per_target, capacity, offset, empty_slot):
    positions, source, target, slot_index, local_block = block_routes(
        parent_blocks, per_source, per_target
    )
    wanted = jnp.arange(per_target, dtype=jnp.int32)
    matches = (target == own_index)[None, :] & (local_block[None, :] == wanted[:, None])
    flat_slot = (source + offset) * capacity + slot_index
    return jnp.where(
        jnp.any(matches, axis=1),
        jnp.sum(jnp.where(matches, flat_slot[None, :], 0), axis=1),
        empty_slot,
    )


def with_zero(blocks, axis):
    shape = list(blocks.shape)
    shape[axis] = 1
    return jnp.concatenate([blocks, jnp.zeros(shape, blocks.dtype)], axis=axis)


def symmetric_of(corner):
    return jnp.tril(corner) + jnp.tril(corner, -1).T


def factor_corner(corner):
    lower = jnp.linalg.cholesky(symmetric_of(corner))
    inverse = jax.scipy.linalg.solve_triangular(
        lower, jnp.eye(PANEL, dtype=jnp.float32), lower=True
    )
    return (lower, inverse)


def apply_inverse(rows, inverse):
    return lax.dot_general(rows, inverse, (((1,), (1,)), ((), ())), precision=lax.Precision.HIGHEST)


def early_corner(child_piece, row_map, col_map, own_diagonal):
    n_row = lax.axis_size("row")
    n_col = lax.axis_size("col")
    n_sub = lax.axis_size("sub")
    rows_here, cols_here = child_piece.shape
    row_blocks = rows_here // BLOCK
    col_blocks = cols_here // BLOCK
    panel_blocks = PANEL // BLOCK
    first_rows = min(row_blocks, -(-panel_blocks // n_row))
    first_cols = min(col_blocks, -(-panel_blocks // n_col))
    piece = child_piece[: first_rows * BLOCK, : first_cols * BLOCK]
    extra = own_diagonal[:PANEL].reshape(-1, first_cols * BLOCK)
    pieces = lax.all_gather(jnp.concatenate([piece, extra], axis=0), ("sub", "row", "col"))
    full_diagonal = pieces[0, first_rows * BLOCK :].reshape(-1)
    pieces = pieces[:, : first_rows * BLOCK]
    pieces = pieces.reshape(n_sub, n_row, n_col, first_rows, BLOCK, first_cols, BLOCK)
    pieces = pieces.transpose(0, 1, 3, 2, 5, 4, 6).reshape(
        n_sub, n_row * first_rows, n_col * first_cols, BLOCK, BLOCK
    )
    row_pos = (
        jnp.arange(n_row, dtype=jnp.int32)[:, None] * row_blocks
        + jnp.arange(first_rows, dtype=jnp.int32)[None, :]
    ).reshape(-1)
    col_pos = (
        jnp.arange(n_col, dtype=jnp.int32)[:, None] * col_blocks
        + jnp.arange(first_cols, dtype=jnp.int32)[None, :]
    ).reshape(-1)
    corner = jnp.zeros((panel_blocks + 1, panel_blocks + 1, BLOCK, BLOCK), jnp.float32)
    for which in range(n_sub):
        rb = row_map[which][row_pos]
        cb = col_map[which][col_pos]
        rb = jnp.where(rb < panel_blocks, rb, panel_blocks)
        cb = jnp.where(cb < panel_blocks, cb, panel_blocks)
        corner = corner.at[rb[:, None], cb[None, :]].add(pieces[which])
    corner = corner[:panel_blocks, :panel_blocks].transpose(0, 2, 1, 3).reshape(PANEL, PANEL)
    return corner + jnp.diag(full_diagonal[:PANEL]), full_diagonal


def shards(child, row_map, col_map, own_diagonal, coupling):
    n_row = lax.axis_size("row")
    n_col = lax.axis_size("col")
    n_group = lax.axis_size(("sub", "col"))
    my_row = lax.axis_index("row")
    my_col = lax.axis_index("col")
    my_sub = lax.axis_index("sub")
    my_group = lax.axis_index(("sub", "col"))
    child_piece = child[0]
    rows_here, cols_here = child_piece.shape
    front_rows = FRONT // n_row
    front_cols = FRONT // n_group
    row_blocks = rows_here // BLOCK
    col_blocks = cols_here // BLOCK
    front_row_blocks = front_rows // BLOCK
    front_col_blocks = front_cols // BLOCK
    row_cap = min(row_blocks, (front_row_blocks + n_row - 1) // n_row)
    col_cap = min(col_blocks, (front_col_blocks + n_col - 1) // n_col)
    n_sub = lax.axis_size("sub")
    my_rows_map = lax.dynamic_index_in_dim(row_map, my_sub, 0, keepdims=False)
    my_cols_map = lax.dynamic_index_in_dim(col_map, my_sub, 0, keepdims=False)

    corner, full_diagonal = early_corner(child_piece, row_map, col_map, own_diagonal)
    global_row = my_row * front_rows + jnp.arange(front_rows, dtype=jnp.int32)

    panel_blocks = PANEL // BLOCK
    first_cols = min(col_blocks, -(-panel_blocks // n_col))
    own_cands = child_piece[:, : first_cols * BLOCK].reshape(row_blocks, BLOCK, first_cols * BLOCK)
    pick_rows = sending_table(my_rows_map, my_row, row_blocks, front_row_blocks, n_row, row_cap)
    pick_rows = jnp.minimum(pick_rows, row_blocks - 1).reshape(n_row, row_cap)
    cand_send = own_cands.at[pick_rows].get(mode="promise_in_bounds")
    pieces = [lax.dynamic_index_in_dim(cand_send, my_row, 0, keepdims=False)]
    for shift in range(1, n_row):
        piece = lax.dynamic_index_in_dim(cand_send, (my_row + shift) % n_row, 0, keepdims=False)
        pieces.append(lax.ppermute(piece, "row", [(i, (i + shift) % n_row) for i in range(n_row)]))
    cand_got = jnp.stack(pieces).reshape(n_row * row_cap, BLOCK, first_cols * BLOCK)
    placement = receiving_table(
        my_rows_map, my_row, row_blocks, front_row_blocks, row_cap, 0, n_row * row_cap
    )
    row_valid = placement < n_row * row_cap
    source = jnp.minimum(placement, n_row * row_cap - 1) // row_cap
    placement = ((my_row - source) % n_row) * row_cap + placement % row_cap
    cand_rows = jnp.where(
        row_valid[:, None, None], cand_got.at[placement].get(mode="promise_in_bounds"), 0.0
    )
    cands = lax.all_gather(cand_rows, "col")
    cands = jnp.stack([cands, lax.ppermute(cands, "sub", [(0, 1), (1, 0)])])
    cands = cands.reshape(n_sub, n_col, front_row_blocks, BLOCK, first_cols, BLOCK)
    cands = cands.transpose(0, 1, 4, 2, 3, 5).reshape(
        n_sub, n_col * first_cols, front_row_blocks, BLOCK, BLOCK
    )
    cand_pos = (
        jnp.arange(n_col, dtype=jnp.int32)[:, None] * col_blocks
        + jnp.arange(first_cols, dtype=jnp.int32)[None, :]
    ).reshape(-1)
    panel_rows = None
    for which in range(n_sub):
        found = col_map[which][cand_pos][None, :] == jnp.arange(panel_blocks, dtype=jnp.int32)[:, None]
        pick = jnp.argmax(found, axis=1)
        mine = lax.dynamic_index_in_dim(cands, (which + my_sub) % n_sub, 0, keepdims=False)
        got = jnp.where(jnp.any(found, axis=1)[:, None, None, None], mine[pick], 0.0)
        panel_rows = got if panel_rows is None else panel_rows + got
    panel_rows = panel_rows.transpose(1, 2, 0, 3).reshape(front_rows, PANEL)
    panel_rows = panel_rows + jnp.where(global_row[:, None] >= PANEL, coupling, 0.0)
    panel_rows = panel_rows + jnp.where(
        global_row[:, None] == jnp.arange(PANEL, dtype=jnp.int32)[None, :], full_diagonal[None, :PANEL], 0.0
    )

    by_col = child_piece.reshape(rows_here, col_blocks, BLOCK)
    chosen = sending_table(my_cols_map, my_col, col_blocks, front_col_blocks, n_group, col_cap)
    chosen = jnp.minimum(chosen, col_blocks - 1).reshape(n_sub, n_col * col_cap)
    chosen = jnp.stack([chosen[1 - my_sub], chosen[my_sub]]).reshape(-1)
    outgoing = by_col.at[:, chosen].get(mode="promise_in_bounds")
    outgoing = outgoing.transpose(1, 0, 2).reshape(2, n_col, col_cap, rows_here, BLOCK)
    outgoing, corner = lax.optimization_barrier((outgoing, corner))
    lower, inverse = factor_corner(corner)
    other_half = lax.all_to_all(outgoing[0], "col", split_axis=0, concat_axis=0, tiled=True)
    other_half, lower, inverse, panel_rows = lax.optimization_barrier(
        (other_half, lower, inverse, panel_rows)
    )
    other_half = lax.ppermute(other_half, "sub", [(0, 1), (1, 0)])

    def row_sending(half, which):
        cols_of = lax.dynamic_index_in_dim(col_map, which, 0, keepdims=False)
        rows_of = lax.dynamic_index_in_dim(row_map, which, 0, keepdims=False)
        col_index = receiving_table(
            cols_of, my_group, col_blocks, front_col_blocks, col_cap, 0, n_col * col_cap
        )
        col_valid = col_index < n_col * col_cap
        col_index = jnp.minimum(col_index, n_col * col_cap - 1)
        row_index = sending_table(rows_of, my_row, row_blocks, front_row_blocks, n_row, row_cap)
        row_index = jnp.minimum(row_index, row_blocks - 1).reshape(n_row, row_cap)
        half = half.reshape(n_col * col_cap, row_blocks, BLOCK, BLOCK)
        sending = half.at[col_index[None, None, :], row_index[:, :, None]].get(
            mode="promise_in_bounds"
        )
        return sending, col_valid, rows_of

    def row_receiving(sending, col_valid, rows_of, by_permutes):
        placement = receiving_table(
            rows_of, my_row, row_blocks, front_row_blocks, row_cap, 0, n_row * row_cap
        )
        row_valid = placement < n_row * row_cap
        placement = jnp.minimum(placement, n_row * row_cap - 1)
        if by_permutes:
            pieces = [lax.dynamic_index_in_dim(sending, my_row, 0, keepdims=False)]
            for shift in range(1, n_row):
                piece = lax.dynamic_index_in_dim(sending, (my_row + shift) % n_row, 0, keepdims=False)
                pairs = [(i, (i + shift) % n_row) for i in range(n_row)]
                pieces.append(lax.ppermute(piece, "row", pairs))
            received = jnp.stack(pieces)
            source = placement // row_cap
            placement = ((my_row - source) % n_row) * row_cap + placement % row_cap
        else:
            received = lax.all_to_all(sending, "row", split_axis=0, concat_axis=0, tiled=True)
        received = received.reshape(n_row * row_cap, front_col_blocks, BLOCK, BLOCK)
        part = received.at[placement].get(mode="promise_in_bounds")
        keep = row_valid[:, None] & col_valid[None, :]
        return part, keep

    sending_other, col_valid_other, rows_other = row_sending(other_half, 1 - my_sub)
    sending_other, own_outgoing = lax.optimization_barrier((sending_other, outgoing[1]))
    part_other, keep_other = row_receiving(sending_other, col_valid_other, rows_other, True)
    own_half = lax.all_to_all(own_outgoing, "col", split_axis=0, concat_axis=0, tiled=True)
    theirs_start = my_group * front_cols % front_rows
    theirs_root = my_group * front_cols // front_rows
    own_rows = apply_inverse(panel_rows, inverse)
    top_rows = jnp.where(my_row == 0, lower, own_rows[:PANEL])
    own_rows = jnp.concatenate([top_rows, own_rows[PANEL:]], axis=0)
    theirs = lax.dynamic_slice_in_dim(own_rows, theirs_start, front_cols, 0)
    theirs = from_root(theirs, "row", theirs_root)
    own_half, part_other, theirs = lax.optimization_barrier((own_half, part_other, theirs))
    sending_own, col_valid_own, rows_own = row_sending(own_half, my_sub)
    part_own, keep_own = row_receiving(sending_own, col_valid_own, rows_own, False)
    assembled = jnp.where(keep_other[:, :, None, None], part_other, 0.0) + jnp.where(
        keep_own[:, :, None, None], part_own, 0.0
    )
    assembled = assembled.transpose(0, 2, 1, 3).reshape(front_rows, front_cols)

    global_col = my_group * front_cols + jnp.arange(front_cols, dtype=jnp.int32)
    on_diagonal = global_row[:, None] == global_col[None, :]
    assembled = assembled + jnp.where(on_diagonal, own_diagonal[None, :], 0.0)
    coupling_wide = jnp.concatenate(
        [coupling, jnp.zeros((front_rows, front_cols - PANEL), jnp.float32)], axis=1
    )
    coupling_mask = (global_row[:, None] >= PANEL) & (global_col[None, :] < PANEL)
    front_part = assembled + jnp.where(coupling_mask, coupling_wide, 0.0)
    update = lax.dot_general(
        own_rows, theirs, (((1,), (1,)), ((), ())), precision=lax.Precision.HIGHEST
    )
    panel_wide = jnp.concatenate(
        [own_rows, jnp.zeros((front_rows, front_cols - PANEL), jnp.float32)], axis=1
    )
    trailing = front_part - update
    result = jnp.where(
        global_col[None, :] < PANEL,
        panel_wide,
        jnp.where(global_row[:, None] < PANEL, 0.0, trailing),
    )
    return result


def solution(mesh):
    placed = (P("sub", "row", "col"), P(), P(), P(("sub", "col")), P("row", None))
    return jax.shard_map(
        shards, mesh=mesh, in_specs=placed, out_specs=P("row", ("sub", "col")), check_vma=False
    )
```
